512 devices in a mesh: pipe: 8 (over x, y_hi), expert: 64 (over z, y_lo, core).
Axes of the slice: x: 4, y: 4 (y_hi: 2, y_lo: 2; y = y_hi * 2 + y_lo), z: 16, core: 2. Of those that a mesh axis runs over, the one named last changes fastest.
Arguments:
- acts_down: bfloat16 [8, 2048, 3584], P('pipe', 'expert'), may hold values from -6 to 6
- routes_down: int32 [8, 2048, 1], P('pipe', 'expert'), may hold values from 0 to 7; in each aligned block of 32 rows (0 to 31, 32 to 63, ..., all dimensions but the last counted through in order) at most 6 rows name the same one
- gates_down: float32 [8, 2048, 1], P('pipe', 'expert'), may hold values from 0.05 to 1
- grads_up: bfloat16 [8, 2048, 3584], P('pipe', 'expert'), may hold values from -6 to 6
- routes_up: int32 [8, 2048, 1], P('pipe', 'expert'), may hold values from 0 to 7; in each aligned block of 32 rows (0 to 31, 32 to 63, ..., all dimensions but the last counted through in order) at most 6 rows name the same one
- gates_up: float32 [8, 2048, 1], P('pipe', 'expert'), may hold values from 0.05 to 1
- weight_in: bfloat16 [8, 64, 448, 2048], P('pipe', 'expert'), may hold values from -0.09375 to 0.09375
- weight_out: bfloat16 [8, 64, 1024, 448], P('pipe', 'expert'), may hold values from -0.1875 to 0.1875
- saved_pre: bfloat16 [8, 64, 48, 2048], P('pipe', 'expert'), may hold values from -5 to 5
Outputs:
- mixed_down: bfloat16 [8, 2048, 3584], P('pipe', 'expert')
- input_grads: bfloat16 [8, 2048, 3584], P('pipe', 'expert')
The draws below stay inside these ranges and needn't reach their ends.
Inputs may be any that keep to these rules, and one draw needn't show every extreme that they name: `routes_down`: each row names one expert. In each aligned block of 32 tokens no expert is named more than 6 times, a bound that some block reaches. `routes_up`: as for routes_down.
All inputs are finite; a program needn't handle non-finite values.
Results may differ from the reference program's by a relative error of at most 0.0034.
Values may be sent and summed in bfloat16 or wider, within the bound.
No kernel may reach another device: no remote copies, remote signals or barrier semaphores. Data moves between devices by JAX's collectives and lax.ppermute only.
A program may use at most 64 MiB of HBM per device.

```python
import math
from functools import partial
import jax
import jax.numpy as jnp
import numpy as np
from jax import lax

D = 3584
FFE = 1024
EXPERTS = 8
TOP = 1
TOK_DEV = 32
SPLIT = 8
MOST = 6
TOKENS = 2048
N_PIPE = 8
N_EXPERT = 64


def block_scale(key, extent, pieces, smallest, largest):
    factor_of = 1.0
    for axis_at, shards_of in pieces:
        draws = jax.random.uniform(jax.random.fold_in(jax.random.fold_in(key, 6), axis_at), (shards_of,), jnp.float32, smallest / len(pieces), largest / len(pieces))
        factor_of = factor_of * jnp.repeat(jnp.exp(draws), extent[axis_at] // shards_of).reshape((-1,) + (1,) * (len(extent) - 1 - axis_at))
    return factor_of


def routed_block(own_key, own, number, rows, count, top, bound, skew):
    ranking = jax.random.permutation(own_key, count)
    crowded, common = shares(count, rows * top, bound, skew, True), shares(count, rows * top, bound, skew, False)
    places = jnp.arange(count)

    def named(tallies, rotation):
        used = int((tallies > 0).sum())
        fixed = max(1, used // 4)
        passed = fixed + (places - fixed + rotation * (used - fixed)) % max(1, count - fixed)
        return jnp.zeros((count,), jnp.int32).at[ranking[jnp.where(places < fixed, places, passed)]].set(jnp.asarray(tallies, jnp.int32))

    tallies = jnp.where(number % 4 == 0, named(crowded, number // 4), named(common, number - number // 4 - 1))
    mixed = jax.random.permutation(jax.random.fold_in(own, 3), count)
    source_of, sink = mixed[0:count // 2 * 2:2], mixed[1:count // 2 * 2:2]
    margin = jnp.minimum(tallies[source_of] - 1, bound - tallies[sink]) // 2
    margin = jnp.where((source_of == ranking[0]) | (sink == ranking[0]) | (tallies[sink] == 0), 0, jnp.maximum(margin, 0))
    passed = jax.random.randint(jax.random.fold_in(own, 4), (count // 2,), 0, 1 << 20) % (margin + 1)
    tallies = tallies.at[source_of].add(-passed).at[sink].add(passed)
    labels = jnp.searchsorted(jnp.cumsum(tallies), jnp.arange(rows * top), side="right").astype(jnp.int32)
    table = labels.reshape(top, rows).T
    table = table[jax.random.permutation(jax.random.fold_in(own, 1), rows)]
    rotation = jax.random.randint(jax.random.fold_in(own, 2), (rows, 1), 0, top)
    return jnp.take_along_axis(table, (jnp.arange(top)[None, :] + rotation) % top, axis=1)


def shares(count, total, most, slope, full):
    portions = [(1 << 20) // math.isqrt(rank ** slope) + 1 for rank in range(1, count + 1)]
    largest = most if full else min(most, max(-(-total // count), total * portions[0] // sum(portions)))
    least = 1 if total - largest >= count - 1 else 0
    counts, spare = [largest] + [least] * (count - 1), total - largest - least * (count - 1)
    while spare > 0:
        movable = [i for i in range(1, count) if counts[i] < largest] or [i for i in range(1, count) if counts[i] < most]
        mass, remaining = sum([portions[i] for i in movable]), spare
        for i in movable:
            more = min(most - counts[i], max(1, remaining * portions[i] // mass), spare)
            counts[i] = counts[i] + more
            spare = spare - more
    return np.array(counts)


def noise(key, extent, spread, most, cuts=(), held_as=jnp.bfloat16):
    array = spread * jax.random.normal(key, extent, jnp.float32)
    if cuts:
        array = array * block_scale(key, extent, cuts, -0.22, 0.18)
    return jnp.clip(array, -most, most).astype(held_as)


def setup_inputs(seed: int = 0) -> dict:
    key_list = jax.random.split(jax.random.key(seed), 10)
    acts_down = noise(key_list[0], (N_PIPE, TOKENS, D), 1.0, 6.0, ((0, 8), (1, 64)))
    routes_down_keys = jax.random.split(jax.random.fold_in(key_list[1], 1), N_PIPE * TOKENS // TOK_DEV)
    routes_down_turns = jax.random.permutation(jax.random.fold_in(key_list[1], 3), N_PIPE * TOKENS // TOK_DEV)
    routes_down = jax.vmap(lambda own, number: routed_block(jax.random.fold_in(key_list[1], 2), own, number, TOK_DEV, EXPERTS, TOP, MOST, 2))(routes_down_keys, routes_down_turns).reshape((N_PIPE, TOKENS, TOP))
    gates_down = jnp.clip(jnp.exp(math.log(1.0) - 2.9957323 * jax.random.uniform(key_list[2], (N_PIPE, TOKENS, TOP), jnp.float32) ** block_scale(key_list[2], (N_PIPE, TOKENS, TOP), ((0, 8), (1, 64)), -0.2, 0.2)), 0.05, 1.0)
    grads_up = noise(key_list[3], (N_PIPE, TOKENS, D), 1.0, 6.0, ((0, 8), (1, 64)))
    routes_up_keys = jax.random.split(jax.random.fold_in(key_list[4], 1), N_PIPE * TOKENS // TOK_DEV)
    routes_up_turns = jax.random.permutation(jax.random.fold_in(key_list[4], 3), N_PIPE * TOKENS // TOK_DEV)
    routes_up = jax.vmap(lambda own, number: routed_block(jax.random.fold_in(key_list[4], 2), own, number, TOK_DEV, EXPERTS, TOP, MOST, 2))(routes_up_keys, routes_up_turns).reshape((N_PIPE, TOKENS, TOP))
    gates_up = jnp.clip(jnp.exp(math.log(1.0) - 2.9957323 * jax.random.uniform(key_list[5], (N_PIPE, TOKENS, TOP), jnp.float32) ** block_scale(key_list[5], (N_PIPE, TOKENS, TOP), ((0, 8), (1, 64)), -0.2, 0.2)), 0.05, 1.0)
    weight_in = noise(key_list[6], (N_PIPE, N_EXPERT, D // SPLIT, 2 * FFE), D ** -0.5, 0.09375, ((0, 8), (1, 64)))
    weight_out = noise(key_list[7], (N_PIPE, N_EXPERT, FFE, D // SPLIT), FFE ** -0.5, 0.1875, ((0, 8), (1, 64)))
    saved_pre = noise(key_list[8], (N_PIPE, N_EXPERT, N_EXPERT * MOST // SPLIT, 2 * FFE), 1.0, 5.0, ((0, 8), (1, 64)))
    return dict(acts_down=acts_down, routes_down=routes_down, gates_down=gates_down, grads_up=grads_up, routes_up=routes_up, gates_up=gates_up, weight_in=weight_in, weight_out=weight_out, saved_pre=saved_pre)


def slot_table(routes, experts, capacity):
    tok_rows, top_count = routes.shape
    flat_routes = routes.reshape(-1)
    onehot = (flat_routes[:, None] == jnp.arange(experts, dtype=jnp.int32)[None, :]).astype(jnp.int32)
    before = jnp.cumsum(onehot, axis=0) - onehot
    rank_within = jnp.sum(before * onehot, axis=1)
    return (flat_routes * capacity + rank_within).reshape(tok_rows, top_count).astype(jnp.int32)


def fill_slots(token_rows, slots, slot_count):
    tok_rows = token_rows.shape[0]
    source = jnp.repeat(jnp.arange(tok_rows, dtype=jnp.int32), slots.shape[1])
    owner_row = jnp.full((slot_count,), tok_rows, dtype=jnp.int32).at[slots.reshape(-1)].set(source)
    padded = jnp.concatenate([token_rows, jnp.zeros((1, token_rows.shape[1]), token_rows.dtype)], axis=0)
    return jnp.take(padded, owner_row, axis=0)


def expert_forward(slot_rows, proj_in, proj_out):
    hidden_units = proj_out.shape[0]
    pre_act = jnp.dot(slot_rows, proj_in, preferred_element_type=jnp.float32)
    hidden = (jax.nn.silu(pre_act[:, :hidden_units]) * pre_act[:, hidden_units:]).astype(jnp.bfloat16)
    return jnp.dot(hidden, proj_out, preferred_element_type=jnp.float32).astype(jnp.bfloat16)


def expert_backward(slot_rows, proj_in, proj_out, saved):
    hidden_units = proj_out.shape[0]
    hidden_grad = lax.dot_general(slot_rows, proj_out, (((1,), (1,)), ((), ())), preferred_element_type=jnp.float32)
    gate_pre = saved[:, :hidden_units].astype(jnp.float32)
    up_pre = saved[:, hidden_units:].astype(jnp.float32)
    sigmoid_gate = jax.nn.sigmoid(gate_pre)
    gate_grad = hidden_grad * up_pre * sigmoid_gate * (1.0 + gate_pre * (1.0 - sigmoid_gate))
    up_grad = hidden_grad * gate_pre * sigmoid_gate
    pre_grad = jnp.concatenate([gate_grad, up_grad], axis=1).astype(jnp.bfloat16)
    return lax.dot_general(pre_grad, proj_in, (((1,), (1,)), ((), ())), preferred_element_type=jnp.float32).astype(jnp.bfloat16)


def combine(token_rows, returned, slots, gates):
    tok_rows, top_count = slots.shape
    gathered = jnp.take(returned, slots.reshape(-1), axis=0).reshape(tok_rows, top_count, returned.shape[1])
    summed = token_rows.astype(jnp.float32) + jnp.einsum("tk,tkd->td", gates.astype(jnp.float32), gathered.astype(jnp.float32))
    return summed.astype(jnp.bfloat16)


def to_owners(blocks):
    return blocks.reshape(N_EXPERT, EXPERTS, MOST, D).transpose(1, 0, 2, 3).reshape(EXPERTS, N_EXPERT * MOST, D)


def to_sources(owned):
    return owned.reshape(EXPERTS, N_EXPERT, MOST, D).transpose(1, 0, 2, 3).reshape(N_EXPERT, EXPERTS * MOST, D)


def owner_forward(owner_args):
    slot_rows, proj_in, proj_out = owner_args
    return expert_forward(slot_rows, proj_in, proj_out)


def owner_backward(owner_args):
    slot_rows, proj_in, proj_out, saved = owner_args
    return expert_backward(slot_rows, proj_in, proj_out, saved)


def one_section(section_args):
    arrived, routes_a, gates_a, incoming, routes_b, gates_b, weight_in_p, weight_out_p, saved_p = section_args
    slot_count = EXPERTS * MOST
    proj_in = weight_in_p.reshape(EXPERTS, D, 2 * FFE)
    proj_out = weight_out_p.reshape(EXPERTS, SPLIT, FFE, D // SPLIT).transpose(0, 2, 1, 3).reshape(EXPERTS, FFE, D)
    saved = saved_p.reshape(EXPERTS, N_EXPERT * MOST, 2 * FFE)
    slotter = partial(slot_table, experts=EXPERTS, capacity=MOST)
    filler = partial(fill_slots, slot_count=slot_count)
    slots_a = jax.vmap(slotter)(routes_a.reshape(N_EXPERT, TOK_DEV, TOP))
    slots_b = jax.vmap(slotter)(routes_b.reshape(N_EXPERT, TOK_DEV, TOP))
    rows_a = arrived.reshape(N_EXPERT, TOK_DEV, D)
    rows_b = incoming.reshape(N_EXPERT, TOK_DEV, D)
    send_a = jax.vmap(filler)(rows_a, slots_a)
    send_b = jax.vmap(filler)(rows_b, slots_b)
    out_a = lax.map(owner_forward, (to_owners(send_a), proj_in, proj_out))
    out_b = lax.map(owner_backward, (to_owners(send_b), proj_in, proj_out, saved))
    mixed_rows = jax.vmap(combine)(rows_a, to_sources(out_a), slots_a, gates_a.reshape(N_EXPERT, TOK_DEV, TOP))
    grad_rows = jax.vmap(combine)(rows_b, to_sources(out_b), slots_b, gates_b.reshape(N_EXPERT, TOK_DEV, TOP))
    return mixed_rows.reshape(TOKENS, D), grad_rows.reshape(TOKENS, D)


def reference(acts_down, routes_down, gates_down, grads_up, routes_up, gates_up, weight_in, weight_out, saved_pre):
    arrived = jnp.roll(acts_down, 1, axis=0)
    incoming = jnp.roll(grads_up, -1, axis=0)
    mixed_down, input_grads = lax.map(one_section, (arrived, routes_down, gates_down, incoming, routes_up, gates_up, weight_in, weight_out, saved_pre))
    return (mixed_down, input_grads)
```

```python
import numpy as np
import jax
import jax.numpy as jnp
from jax import lax
from jax.sharding import PartitionSpec as P

EXPERTS = 8
MOST = 6


def shifted(block, axis, distance):
    devices = range(lax.axis_size(axis))
    route = [((i - distance) % len(devices), i) for i in devices]
    return lax.ppermute(block, axis, route)


def slot_table(routes, experts, capacity):
    tok_rows, top_count = routes.shape
    flat_routes = routes.reshape(-1)
    onehot = (flat_routes[:, None] == jnp.arange(experts, dtype=jnp.int32)[None, :]).astype(
        jnp.int32
    )
    before = jnp.cumsum(onehot, axis=0) - onehot
    rank_within = jnp.sum(before * onehot, axis=1)
    return (flat_routes * capacity + rank_within).reshape(tok_rows, top_count)


def fill_slots(token_rows, slots, slot_count):
    tok_rows = token_rows.shape[0]
    source = jnp.repeat(jnp.arange(tok_rows, dtype=jnp.int32), slots.shape[1])
    owner_row = jnp.full((slot_count,), tok_rows, dtype=jnp.int32).at[slots.reshape(-1)].set(source)
    padded = jnp.concatenate(
        [token_rows, jnp.zeros((1, token_rows.shape[1]), token_rows.dtype)], axis=0
    )
    return jnp.take(padded, owner_row, axis=0)


def stage_bits(member_bits):
    core = member_bits[0]
    return [
        0,
        1 if core == 0 else 2,
        2 if core == 0 else 1,
    ]


def member_bits_of(member, group_size):
    return [member >> b & 1 for b in range(group_size.bit_length() - 1)]


def stage_route(axis_count, group_size, stage):
    route = []
    for index in range(axis_count):
        bits = member_bits_of(index % group_size, group_size)
        bit = stage_bits(bits)[stage]
        route.append((index, index ^ (1 << bit)))
    return route


def block_order(group_size):
    levels = group_size.bit_length() - 1
    order = [0] * group_size
    for member in range(group_size):
        bits = member_bits_of(member, group_size)
        pos = 0
        for bit in stage_bits(bits):
            pos = pos * 2 + bits[bit]
        order[pos] = member
    assert levels == 3
    return np.array(order)


def own_stage_bit(index, group_size, stage):
    member = index % group_size
    core = member & 1
    if stage == 0:
        bit = 0
    elif stage == 1:
        bit = jnp.where(core == 0, 1, 2)
    else:
        bit = jnp.where(core == 0, 2, 1)
    return (member >> bit & 1) == 1


def share_sum(partial_sums, index, group_size, axis_count):
    current = partial_sums
    for stage in range(group_size.bit_length() - 1):
        half_rows = current.shape[0] // 2
        lower_half = current[:half_rows]
        upper_half = current[half_rows:]
        high_bit = own_stage_bit(index, group_size, stage)
        kept_part = jnp.where(high_bit, upper_half, lower_half)
        sent_part = jnp.where(high_bit, lower_half, upper_half)
        route = stage_route(axis_count, group_size, stage)
        current = kept_part + lax.ppermute(sent_part, "expert", route)
    return current


def share_gather(piece, index, group_size, axis_count):
    current = piece
    for stage in reversed(range(group_size.bit_length() - 1)):
        route = stage_route(axis_count, group_size, stage)
        partner_rows = lax.ppermute(current, "expert", route)
        high_bit = own_stage_bit(index, group_size, stage)
        current = jnp.where(
            high_bit,
            jnp.concatenate([partner_rows, current], axis=0),
            jnp.concatenate([current, partner_rows], axis=0),
        )
    return current


def combine(token_rows, returned, slots, gates):
    tok_rows, top_count = slots.shape
    gathered = jnp.take(returned, slots.reshape(-1), axis=0).reshape(
        tok_rows, top_count, returned.shape[1]
    )
    summed = token_rows.astype(jnp.float32) + jnp.einsum(
        "tk,tkd->td", gates, gathered.astype(jnp.float32)
    )
    return summed.astype(jnp.bfloat16)


def body(
    acts_down,
    routes_down,
    gates_down,
    grads_up,
    routes_up,
    gates_up,
    weight_in,
    weight_out,
    saved_pre,
):
    devices = lax.axis_size("expert")
    group_size = devices // EXPERTS
    index = lax.axis_index("expert")
    model_width = acts_down.shape[2]
    share_width = model_width // group_size
    slot_count = EXPERTS * MOST
    proj_in = weight_in[0, 0]
    proj_out = weight_out[0, 0]
    saved = saved_pre[0, 0]
    hidden_units = proj_out.shape[0]
    order = block_order(group_size)
    unorder = np.argsort(order)

    def to_devices(full_rows):
        return (
            full_rows.reshape(EXPERTS, MOST, group_size, share_width)
            .transpose(0, 2, 1, 3)
            .reshape(devices, MOST, share_width)
        )

    def from_devices(returned):
        return (
            returned.reshape(EXPERTS, group_size, MOST, share_width)
            .transpose(0, 2, 1, 3)
            .reshape(slot_count, model_width)
        )

    def reorder(rows, perm):
        blocks = rows.reshape(group_size, -1, rows.shape[-1])
        return jnp.concatenate([blocks[k] for k in perm], axis=0)

    arrived = shifted(acts_down[0], "pipe", 1)
    incoming = shifted(grads_up[0], "pipe", -1)
    slots_down = slot_table(routes_down[0], EXPERTS, MOST)
    slots_up = slot_table(routes_up[0], EXPERTS, MOST)
    send_down = to_devices(fill_slots(arrived, slots_down, slot_count))
    send_up = to_devices(fill_slots(incoming, slots_up, slot_count))
    sent = jnp.stack([send_down, send_up], axis=1)
    got = lax.all_to_all(sent, "expert", split_axis=0, concat_axis=0, tiled=True)
    rows_down = got[:, 0].reshape(-1, share_width)
    rows_up = reorder(got[:, 1].reshape(-1, share_width), order)

    partial_pre = jnp.dot(rows_down, proj_in, preferred_element_type=jnp.float32)
    partial_grad = lax.dot_general(
        rows_up, proj_out, (((1,), (1,)), ((), ())), preferred_element_type=jnp.float32
    )
    summed = share_sum(
        jnp.concatenate([partial_pre, partial_grad], axis=1), index, group_size, devices
    )
    pre_share = summed[:, : 2 * hidden_units]
    hidden_grad = summed[:, 2 * hidden_units :]
    hidden_share = (
        jax.nn.silu(pre_share[:, :hidden_units]) * pre_share[:, hidden_units:]
    ).astype(jnp.bfloat16)
    gate_pre = saved[:, :hidden_units].astype(jnp.float32)
    up_pre = saved[:, hidden_units:].astype(jnp.float32)
    sigmoid_gate = jax.nn.sigmoid(gate_pre)
    gate_grad = hidden_grad * up_pre * sigmoid_gate * (1.0 + gate_pre * (1.0 - sigmoid_gate))
    up_grad = hidden_grad * gate_pre * sigmoid_gate
    grad_share = jnp.concatenate([gate_grad, up_grad], axis=1).astype(jnp.bfloat16)
    gathered = share_gather(
        jnp.concatenate([hidden_share, grad_share], axis=1), index, group_size, devices
    )
    hidden = gathered[:, :hidden_units]
    pre_grad = gathered[:, hidden_units:]
    out_down = jnp.dot(hidden, proj_out, preferred_element_type=jnp.float32).astype(
        jnp.bfloat16
    )
    out_up = lax.dot_general(
        pre_grad, proj_in, (((1,), (1,)), ((), ())), preferred_element_type=jnp.float32
    ).astype(jnp.bfloat16)
    out_up = reorder(out_up, unorder)
    result = jnp.stack(
        [out_down.reshape(devices, MOST, share_width), out_up.reshape(devices, MOST, share_width)],
        axis=1,
    )
    back = lax.all_to_all(result, "expert", split_axis=0, concat_axis=0, tiled=True)
    mixed_rows = combine(arrived, from_devices(back[:, 0]), slots_down, gates_down[0])
    grad_rows = combine(incoming, from_devices(back[:, 1]), slots_up, gates_up[0])
    return (mixed_rows[None], grad_rows[None])


def solution(mesh):
    placed = (
        P("pipe", "expert", None),
        P("pipe", "expert", None),
        P("pipe", "expert", None),
        P("pipe", "expert", None),
        P("pipe", "expert", None),
        P("pipe", "expert", None),
        P("pipe", "expert", None, None),
        P("pipe", "expert", None, None),
        P("pipe", "expert", None, None),
    )
    return jax.shard_map(
        body,
        mesh=mesh,
        in_specs=placed,
        out_specs=(P("pipe", "expert", None), P("pipe", "expert", None)),
        check_vma=False,
    )
```

```python
import numpy as np
import jax
import jax.numpy as jnp
from jax import lax
from jax.sharding import PartitionSpec as P

EXPERTS = 8
MOST = 6


def shifted(block, axis, distance):
    devices = range(lax.axis_size(axis))
    route = [((i - distance) % len(devices), i) for i in devices]
    return lax.ppermute(block, axis, route)


def slot_tables(routes, experts, capacity):
    paths, tok_rows, top_count = routes.shape
    flat = routes.reshape(paths, tok_rows * top_count)
    pairs = flat.shape[1]
    earlier = jnp.arange(pairs)[None, :] < jnp.arange(pairs)[:, None]
    same = (flat[:, :, None] == flat[:, None, :]) & earlier[None]
    rank_within = jnp.sum(same.astype(jnp.int32), axis=2)
    return (flat * capacity + rank_within).reshape(paths, tok_rows, top_count)


def stage_bits(member_bits):
    core = member_bits[0]
    return [0, 1 if core == 0 else 2, 2 if core == 0 else 1]


def member_bits_of(member, group_size):
    return [member >> b & 1 for b in range(group_size.bit_length() - 1)]


def stage_route(axis_count, group_size, stage):
    route = []
    for index in range(axis_count):
        bits = member_bits_of(index % group_size, group_size)
        bit = stage_bits(bits)[stage]
        route.append((index, index ^ (1 << bit)))
    return route


def block_order(group_size):
    order = [0] * group_size
    for member in range(group_size):
        bits = member_bits_of(member, group_size)
        pos = 0
        for bit in stage_bits(bits):
            pos = pos * 2 + bits[bit]
        order[pos] = member
    return order


def own_stage_bit(index, group_size, stage):
    member = index % group_size
    core = member & 1
    if stage == 0:
        bit = 0
    elif stage == 1:
        bit = jnp.where(core == 0, 1, 2)
    else:
        bit = jnp.where(core == 0, 2, 1)
    return (member >> bit & 1).astype(jnp.int32)


def body(
    acts_down,
    routes_down,
    gates_down,
    grads_up,
    routes_up,
    gates_up,
    weight_in,
    weight_out,
    saved_pre,
):
    devices = lax.axis_size("expert")
    group_size = devices // EXPERTS
    levels = group_size.bit_length() - 1
    index = lax.axis_index("expert")
    model_width = acts_down.shape[2]
    share_width = model_width // group_size
    slot_count = EXPERTS * MOST
    proj_in = weight_in[0, 0]
    proj_out = weight_out[0, 0]
    hidden_units = proj_out.shape[0]
    order = block_order(group_size)

    saved_route = [
        (i, (i // group_size) * group_size + order[i % group_size]) for i in range(devices)
    ]
    saved = lax.ppermute(saved_pre[0, 0], "expert", saved_route)

    arrived = shifted(acts_down[0], "pipe", 1)
    incoming = shifted(grads_up[0], "pipe", -1)
    tokens = jnp.stack([arrived, incoming])
    routes = jnp.stack([routes_down[0], routes_up[0]])
    gates = jnp.stack([gates_down[0], gates_up[0]]).astype(jnp.float32)
    slots = slot_tables(routes, EXPERTS, MOST)
    onehot = (
        slots.transpose(0, 2, 1)[:, :, None, :]
        == jnp.arange(slot_count, dtype=jnp.int32)[None, None, :, None]
    ).astype(jnp.bfloat16)
    dispatch = jnp.sum(onehot, axis=1).reshape(2, EXPERTS, MOST, -1)
    token_parts = tokens.reshape(2, tokens.shape[1], group_size, share_width)
    sent = jnp.einsum(
        "prjt,pthc->rhpjc", dispatch, token_parts, preferred_element_type=jnp.float32
    ).astype(jnp.bfloat16)
    sent = sent.reshape(devices, 2, MOST, share_width)
    got = lax.all_to_all(sent, "expert", split_axis=0, concat_axis=0, tiled=True)
    rows_down = got[:, 0].reshape(-1, share_width)
    rows_up = got[:, 1].reshape(-1, share_width)

    def first_partial(start, count):
        part_down = lax.dynamic_slice_in_dim(rows_down, start, count, axis=0)
        part_up = lax.dynamic_slice_in_dim(rows_up, start, count, axis=0)
        pre = jnp.dot(part_down, proj_in, preferred_element_type=jnp.float32)
        grad = lax.dot_general(
            part_up, proj_out, (((1,), (1,)), ((), ())), preferred_element_type=jnp.float32
        )
        return jnp.concatenate([pre, grad], axis=1)

    half = rows_down.shape[0] // 2
    bit = own_stage_bit(index, group_size, 0)
    send_part = first_partial((1 - bit) * half, half)
    received = lax.ppermute(send_part, "expert", stage_route(devices, group_size, 0))
    current = first_partial(bit * half, half) + received
    for stage in range(1, levels):
        half = current.shape[0] // 2
        bit = own_stage_bit(index, group_size, stage)
        kept = lax.dynamic_slice_in_dim(current, bit * half, half, axis=0)
        send_part = lax.dynamic_slice_in_dim(current, (1 - bit) * half, half, axis=0)
        received = lax.ppermute(send_part, "expert", stage_route(devices, group_size, stage))
        current = kept + received

    pre_share = current[:, : 2 * hidden_units]
    hidden_grad = current[:, 2 * hidden_units :]
    hidden_share = (
        jax.nn.silu(pre_share[:, :hidden_units]) * pre_share[:, hidden_units:]
    ).astype(jnp.bfloat16)
    gate_pre = saved[:, :hidden_units].astype(jnp.float32)
    up_pre = saved[:, hidden_units:].astype(jnp.float32)
    sigmoid_gate = jax.nn.sigmoid(gate_pre)
    gate_grad = hidden_grad * up_pre * sigmoid_gate * (1.0 + gate_pre * (1.0 - sigmoid_gate))
    up_grad = hidden_grad * gate_pre * sigmoid_gate
    current = jnp.concatenate([hidden_share, gate_grad.astype(jnp.bfloat16), up_grad.astype(jnp.bfloat16)], axis=1)

    for stage in reversed(range(1, levels)):
        bit = own_stage_bit(index, group_size, stage)
        partner = lax.ppermute(current, "expert", stage_route(devices, group_size, stage))
        current = jnp.where(
            bit == 1,
            jnp.concatenate([partner, current], axis=0),
            jnp.concatenate([current, partner], axis=0),
        )

    def last_matmul(block):
        out_down = jnp.dot(
            block[:, :hidden_units], proj_out, preferred_element_type=jnp.float32
        ).astype(jnp.bfloat16)
        out_up = lax.dot_general(
            block[:, hidden_units:], proj_in, (((1,), (1,)), ((), ())),
            preferred_element_type=jnp.float32,
        ).astype(jnp.bfloat16)
        return jnp.stack([out_down, out_up])

    bit = own_stage_bit(index, group_size, 0)
    partner = lax.ppermute(current, "expert", stage_route(devices, group_size, 0))
    own_out = last_matmul(current)
    partner_out = last_matmul(partner)
    result = jnp.where(
        bit == 1,
        jnp.concatenate([partner_out, own_out], axis=1),
        jnp.concatenate([own_out, partner_out], axis=1),
    )
    result = result.reshape(2, devices, MOST, share_width).transpose(1, 0, 2, 3)
    back = lax.all_to_all(result, "expert", split_axis=0, concat_axis=0, tiled=True)
    back = back.reshape(EXPERTS, group_size, 2, MOST, share_width)
    gathered = jnp.einsum(
        "pkrjt,rhpjc->ptkhc",
        onehot.reshape(2, -1, EXPERTS, MOST, onehot.shape[-1]),
        back,
        preferred_element_type=jnp.float32,
    )
    gathered = gathered.reshape(2, tokens.shape[1], -1, model_width)
    summed = tokens.astype(jnp.float32) + jnp.sum(gates[..., None] * gathered, axis=2)
    summed = summed.astype(jnp.bfloat16)
    return (summed[0][None], summed[1][None])


def solution(mesh):
    placed = (
        P("pipe", "expert", None),
        P("pipe", "expert", None),
        P("pipe", "expert", None),
        P("pipe", "expert", None),
        P("pipe", "expert", None),
        P("pipe", "expert", None),
        P("pipe", "expert", None, None),
        P("pipe", "expert", None, None),
        P("pipe", "expert", None, None),
    )
    return jax.shard_map(
        body,
        mesh=mesh,
        in_specs=placed,
        out_specs=(P("pipe", "expert", None), P("pipe", "expert", None)),
        check_vma=False,
    )
```

```python
import numpy as np
import jax
import jax.numpy as jnp
from jax import lax
from jax.sharding import PartitionSpec as P

EXPERTS = 8
MOST = 6


def shifted(block, axis, distance):
    devices = range(lax.axis_size(axis))
    route = [((i - distance) % len(devices), i) for i in devices]
    return lax.ppermute(block, axis, route)


def slot_tables(routes, experts, capacity):
    paths, tok_rows, top_count = routes.shape
    flat = routes.reshape(paths, tok_rows * top_count)
    pairs = flat.shape[1]
    earlier = jnp.arange(pairs)[None, :] < jnp.arange(pairs)[:, None]
    same = (flat[:, :, None] == flat[:, None, :]) & earlier[None]
    rank_within = jnp.sum(same.astype(jnp.int32), axis=2)
    return (flat * capacity + rank_within).reshape(paths, tok_rows, top_count)


def stage_bits(member_bits):
    core = member_bits[0]
    return [0, 1 if core == 0 else 2, 2 if core == 0 else 1]


def member_bits_of(member, group_size):
    return [member >> b & 1 for b in range(group_size.bit_length() - 1)]


def stage_route(axis_count, group_size, stage):
    route = []
    for index in range(axis_count):
        bits = member_bits_of(index % group_size, group_size)
        bit = stage_bits(bits)[stage]
        route.append((index, index ^ (1 << bit)))
    return route


def block_order(group_size):
    order = [0] * group_size
    for member in range(group_size):
        bits = member_bits_of(member, group_size)
        pos = 0
        for bit in stage_bits(bits):
            pos = pos * 2 + bits[bit]
        order[pos] = member
    return order


def own_stage_bit(index, group_size, stage):
    member = index % group_size
    core = member & 1
    if stage == 0:
        bit = 0
    elif stage == 1:
        bit = jnp.where(core == 0, 1, 2)
    else:
        bit = jnp.where(core == 0, 2, 1)
    return (member >> bit & 1).astype(jnp.int32)


def body(
    acts_down,
    routes_down,
    gates_down,
    grads_up,
    routes_up,
    gates_up,
    weight_in,
    weight_out,
    saved_pre,
):
    devices = lax.axis_size("expert")
    group_size = devices // EXPERTS
    levels = group_size.bit_length() - 1
    index = lax.axis_index("expert")
    model_width = acts_down.shape[2]
    share_width = model_width // group_size
    slot_count = EXPERTS * MOST
    proj_in = weight_in[0, 0]
    proj_out = weight_out[0, 0]
    hidden_units = proj_out.shape[0]
    order = block_order(group_size)

    saved_route = [
        (i, (i // group_size) * group_size + order[i % group_size]) for i in range(devices)
    ]
    saved = lax.ppermute(saved_pre[0, 0], "expert", saved_route)

    arrived = shifted(acts_down[0], "pipe", 1)
    incoming = shifted(grads_up[0], "pipe", -1)
    tokens = jnp.stack([arrived, incoming])
    routes = jnp.stack([routes_down[0], routes_up[0]])
    gates = jnp.stack([gates_down[0], gates_up[0]]).astype(jnp.float32)
    slots = slot_tables(routes, EXPERTS, MOST)
    onehot = (
        slots.transpose(0, 2, 1)[:, :, None, :]
        == jnp.arange(slot_count, dtype=jnp.int32)[None, None, :, None]
    ).astype(jnp.bfloat16)
    dispatch = jnp.sum(onehot, axis=1).reshape(2, EXPERTS, MOST, -1)
    token_parts = tokens.reshape(2, tokens.shape[1], group_size, share_width)
    sent = jnp.einsum(
        "prjt,pthc->rhpjc", dispatch, token_parts, preferred_element_type=jnp.float32
    ).astype(jnp.bfloat16)
    sent = sent.reshape(devices, 2, MOST, share_width)
    got = lax.all_to_all(sent, "expert", split_axis=0, concat_axis=0, tiled=True)
    rows_down = got[:, 0].reshape(-1, share_width)
    rows_up = got[:, 1].reshape(-1, share_width)

    def first_partial(start, count):
        part_down = lax.dynamic_slice_in_dim(rows_down, start, count, axis=0)
        part_up = lax.dynamic_slice_in_dim(rows_up, start, count, axis=0)
        pre = jnp.dot(part_down, proj_in, preferred_element_type=jnp.float32)
        grad = lax.dot_general(
            part_up, proj_out, (((1,), (1,)), ((), ())), preferred_element_type=jnp.float32
        )
        return jnp.concatenate([pre, grad], axis=1)

    half = rows_down.shape[0] // 2
    bit = own_stage_bit(index, group_size, 0)
    send_part = first_partial((1 - bit) * half, half).astype(jnp.bfloat16)
    received = lax.ppermute(send_part, "expert", stage_route(devices, group_size, 0))
    current = first_partial(bit * half, half) + received.astype(jnp.float32)
    for stage in range(1, levels):
        half = current.shape[0] // 2
        bit = own_stage_bit(index, group_size, stage)
        kept = lax.dynamic_slice_in_dim(current, bit * half, half, axis=0)
        send_part = lax.dynamic_slice_in_dim(current, (1 - bit) * half, half, axis=0)
        send_part = send_part.astype(jnp.bfloat16)
        received = lax.ppermute(send_part, "expert", stage_route(devices, group_size, stage))
        current = kept + received.astype(jnp.float32)

    pre_share = current[:, : 2 * hidden_units]
    hidden_grad = current[:, 2 * hidden_units :]
    hidden_share = (
        jax.nn.silu(pre_share[:, :hidden_units]) * pre_share[:, hidden_units:]
    ).astype(jnp.bfloat16)
    gate_pre = saved[:, :hidden_units].astype(jnp.float32)
    up_pre = saved[:, hidden_units:].astype(jnp.float32)
    sigmoid_gate = jax.nn.sigmoid(gate_pre)
    gate_grad = hidden_grad * up_pre * sigmoid_gate * (1.0 + gate_pre * (1.0 - sigmoid_gate))
    up_grad = hidden_grad * gate_pre * sigmoid_gate
    current = jnp.concatenate([hidden_share, gate_grad.astype(jnp.bfloat16), up_grad.astype(jnp.bfloat16)], axis=1)

    for stage in reversed(range(1, levels)):
        bit = own_stage_bit(index, group_size, stage)
        partner = lax.ppermute(current, "expert", stage_route(devices, group_size, stage))
        current = jnp.where(
            bit == 1,
            jnp.concatenate([partner, current], axis=0),
            jnp.concatenate([current, partner], axis=0),
        )

    def last_matmul(block):
        out_down = jnp.dot(
            block[:, :hidden_units], proj_out, preferred_element_type=jnp.float32
        ).astype(jnp.bfloat16)
        out_up = lax.dot_general(
            block[:, hidden_units:], proj_in, (((1,), (1,)), ((), ())),
            preferred_element_type=jnp.float32,
        ).astype(jnp.bfloat16)
        return jnp.stack([out_down, out_up])

    bit = own_stage_bit(index, group_size, 0)
    partner = lax.ppermute(current, "expert", stage_route(devices, group_size, 0))
    own_out = last_matmul(current)
    partner_out = last_matmul(partner)
    result = jnp.where(
        bit == 1,
        jnp.concatenate([partner_out, own_out], axis=1),
        jnp.concatenate([own_out, partner_out], axis=1),
    )
    result = result.reshape(2, devices, MOST, share_width).transpose(1, 0, 2, 3)
    back = lax.all_to_all(result, "expert", split_axis=0, concat_axis=0, tiled=True)
    back = back.reshape(EXPERTS, group_size, 2, MOST, share_width)
    gathered = jnp.einsum(
        "pkrjt,rhpjc->ptkhc",
        onehot.reshape(2, -1, EXPERTS, MOST, onehot.shape[-1]),
        back,
        preferred_element_type=jnp.float32,
    )
    gathered = gathered.reshape(2, tokens.shape[1], -1, model_width)
    summed = tokens.astype(jnp.float32) + jnp.sum(gates[..., None] * gathered, axis=2)
    summed = summed.astype(jnp.bfloat16)
    return (summed[0][None], summed[1][None])


def solution(mesh):
    placed = (
        P("pipe", "expert", None),
        P("pipe", "expert", None),
        P("pipe", "expert", None),
        P("pipe", "expert", None),
        P("pipe", "expert", None),
        P("pipe", "expert", None),
        P("pipe", "expert", None, None),
        P("pipe", "expert", None, None),
        P("pipe", "expert", None, None),
    )
    return jax.shard_map(
        body,
        mesh=mesh,
        in_specs=placed,
        out_specs=(P("pipe", "expert", None), P("pipe", "expert", None)),
        check_vma=False,
    )
```

```python
import numpy as np
import jax
import jax.numpy as jnp
from jax import lax
from jax.sharding import PartitionSpec as P

EXPERTS = 8
MOST = 6


def shifted(block, axis, distance):
    devices = range(lax.axis_size(axis))
    route = [((i - distance) % len(devices), i) for i in devices]
    return lax.ppermute(block, axis, route)


def slot_tables(routes, experts, capacity):
    paths, tok_rows, top_count = routes.shape
    flat = routes.reshape(paths, tok_rows * top_count)
    pairs = flat.shape[1]
    earlier = jnp.arange(pairs)[None, :] < jnp.arange(pairs)[:, None]
    same = (flat[:, :, None] == flat[:, None, :]) & earlier[None]
    rank_within = jnp.sum(same.astype(jnp.int32), axis=2)
    return (flat * capacity + rank_within).reshape(paths, tok_rows, top_count)


def stage_bits(member_bits):
    core = member_bits[0]
    return [0, 1 if core == 0 else 2, 2 if core == 0 else 1]


def member_bits_of(member, group_size):
    return [member >> b & 1 for b in range(group_size.bit_length() - 1)]


def stage_route(axis_count, group_size, stage):
    route = []
    for index in range(axis_count):
        bits = member_bits_of(index % group_size, group_size)
        bit = stage_bits(bits)[stage]
        route.append((index, index ^ (1 << bit)))
    return route


def block_order(group_size):
    order = [0] * group_size
    for member in range(group_size):
        bits = member_bits_of(member, group_size)
        pos = 0
        for bit in stage_bits(bits):
            pos = pos * 2 + bits[bit]
        order[pos] = member
    return order


def own_stage_bit(index, group_size, stage):
    member = index % group_size
    core = member & 1
    if stage == 0:
        bit = 0
    elif stage == 1:
        bit = jnp.where(core == 0, 1, 2)
    else:
        bit = jnp.where(core == 0, 2, 1)
    return (member >> bit & 1).astype(jnp.int32)


def encode_rows(values, lanes):
    largest = jnp.maximum(jnp.max(jnp.abs(values), axis=1, keepdims=True), 1e-30)
    exponent = jnp.floor(jnp.log2(largest)) - 13.0
    coded = jnp.round(values * jnp.exp2(-exponent)).astype(jnp.int16)
    tail = jnp.broadcast_to(exponent.astype(jnp.int16), (values.shape[0], lanes))
    return jnp.concatenate([coded, tail], axis=1)


def decode_rows(coded, width):
    exponent = coded[:, width : width + 1].astype(jnp.float32)
    return coded[:, :width].astype(jnp.float32) * jnp.exp2(exponent)


def body(
    acts_down,
    routes_down,
    gates_down,
    grads_up,
    routes_up,
    gates_up,
    weight_in,
    weight_out,
    saved_pre,
):
    devices = lax.axis_size("expert")
    group_size = devices // EXPERTS
    levels = group_size.bit_length() - 1
    index = lax.axis_index("expert")
    model_width = acts_down.shape[2]
    share_width = model_width // group_size
    slot_count = EXPERTS * MOST
    proj_in = weight_in[0, 0]
    proj_out = weight_out[0, 0]
    hidden_units = proj_out.shape[0]
    order = block_order(group_size)

    saved_route = [
        (i, (i // group_size) * group_size + order[i % group_size]) for i in range(devices)
    ]
    saved = lax.ppermute(saved_pre[0, 0], "expert", saved_route)

    arrived = shifted(acts_down[0], "pipe", 1)
    incoming = shifted(grads_up[0], "pipe", -1)
    tokens = jnp.stack([arrived, incoming])
    routes = jnp.stack([routes_down[0], routes_up[0]])
    gates = jnp.stack([gates_down[0], gates_up[0]]).astype(jnp.float32)
    slots = slot_tables(routes, EXPERTS, MOST)
    onehot = (
        slots.transpose(0, 2, 1)[:, :, None, :]
        == jnp.arange(slot_count, dtype=jnp.int32)[None, None, :, None]
    ).astype(jnp.bfloat16)
    dispatch = jnp.sum(onehot, axis=1).reshape(2, EXPERTS, MOST, -1)
    token_parts = tokens.reshape(2, tokens.shape[1], group_size, share_width)
    sent = jnp.einsum(
        "prjt,pthc->rhpjc", dispatch, token_parts, preferred_element_type=jnp.float32
    ).astype(jnp.bfloat16)
    sent = sent.reshape(devices, 2, MOST, share_width)
    got = lax.all_to_all(sent, "expert", split_axis=0, concat_axis=0, tiled=True)
    rows_down = got[:, 0].reshape(-1, share_width)
    rows_up = got[:, 1].reshape(-1, share_width)

    def first_partial(start, count):
        part_down = lax.dynamic_slice_in_dim(rows_down, start, count, axis=0)
        part_up = lax.dynamic_slice_in_dim(rows_up, start, count, axis=0)
        pre = jnp.dot(part_down, proj_in, preferred_element_type=jnp.float32)
        grad = lax.dot_general(
            part_up, proj_out, (((1,), (1,)), ((), ())), preferred_element_type=jnp.float32
        )
        return jnp.concatenate([pre, grad], axis=1)

    half = rows_down.shape[0] // 2
    bit = own_stage_bit(index, group_size, 0)
    send_part = first_partial((1 - bit) * half, half)
    received = lax.ppermute(send_part, "expert", stage_route(devices, group_size, 0))
    current = first_partial(bit * half, half) + received
    for stage in range(1, levels):
        half = current.shape[0] // 2
        bit = own_stage_bit(index, group_size, stage)
        kept = lax.dynamic_slice_in_dim(current, bit * half, half, axis=0)
        send_part = lax.dynamic_slice_in_dim(current, (1 - bit) * half, half, axis=0)
        width = send_part.shape[1]
        received = lax.ppermute(
            encode_rows(send_part, 128), "expert", stage_route(devices, group_size, stage)
        )
        current = kept + decode_rows(received, width)

    pre_share = current[:, : 2 * hidden_units]
    hidden_grad = current[:, 2 * hidden_units :]
    hidden_share = (
        jax.nn.silu(pre_share[:, :hidden_units]) * pre_share[:, hidden_units:]
    ).astype(jnp.bfloat16)
    gate_pre = saved[:, :hidden_units].astype(jnp.float32)
    up_pre = saved[:, hidden_units:].astype(jnp.float32)
    sigmoid_gate = jax.nn.sigmoid(gate_pre)
    gate_grad = hidden_grad * up_pre * sigmoid_gate * (1.0 + gate_pre * (1.0 - sigmoid_gate))
    up_grad = hidden_grad * gate_pre * sigmoid_gate
    current = jnp.concatenate([hidden_share, gate_grad.astype(jnp.bfloat16), up_grad.astype(jnp.bfloat16)], axis=1)

    for stage in reversed(range(1, levels)):
        bit = own_stage_bit(index, group_size, stage)
        partner = lax.ppermute(current, "expert", stage_route(devices, group_size, stage))
        current = jnp.where(
            bit == 1,
            jnp.concatenate([partner, current], axis=0),
            jnp.concatenate([current, partner], axis=0),
        )

    def last_matmul(block):
        out_down = jnp.dot(
            block[:, :hidden_units], proj_out, preferred_element_type=jnp.float32
        ).astype(jnp.bfloat16)
        out_up = lax.dot_general(
            block[:, hidden_units:], proj_in, (((1,), (1,)), ((), ())),
            preferred_element_type=jnp.float32,
        ).astype(jnp.bfloat16)
        return jnp.stack([out_down, out_up])

    bit = own_stage_bit(index, group_size, 0)
    partner = lax.ppermute(current, "expert", stage_route(devices, group_size, 0))
    own_out = last_matmul(current)
    partner_out = last_matmul(partner)
    result = jnp.where(
        bit == 1,
        jnp.concatenate([partner_out, own_out], axis=1),
        jnp.concatenate([own_out, partner_out], axis=1),
    )
    result = result.reshape(2, devices, MOST, share_width).transpose(1, 0, 2, 3)
    back = lax.all_to_all(result, "expert", split_axis=0, concat_axis=0, tiled=True)
    back = back.reshape(EXPERTS, group_size, 2, MOST, share_width)
    gathered = jnp.einsum(
        "pkrjt,rhpjc->ptkhc",
        onehot.reshape(2, -1, EXPERTS, MOST, onehot.shape[-1]),
        back,
        preferred_element_type=jnp.float32,
    )
    gathered = gathered.reshape(2, tokens.shape[1], -1, model_width)
    summed = tokens.astype(jnp.float32) + jnp.sum(gates[..., None] * gathered, axis=2)
    summed = summed.astype(jnp.bfloat16)
    return (summed[0][None], summed[1][None])


def solution(mesh):
    placed = (
        P("pipe", "expert", None),
        P("pipe", "expert", None),
        P("pipe", "expert", None),
        P("pipe", "expert", None),
        P("pipe", "expert", None),
        P("pipe", "expert", None),
        P("pipe", "expert", None, None),
        P("pipe", "expert", None, None),
        P("pipe", "expert", None, None),
    )
    return jax.shard_map(
        body,
        mesh=mesh,
        in_specs=placed,
        out_specs=(P("pipe", "expert", None), P("pipe", "expert", None)),
        check_vma=False,
    )
```

```python
import numpy as np
import jax
import jax.numpy as jnp
from jax import lax
from jax.sharding import PartitionSpec as P

EXPERTS = 8
MOST = 6


def shifted(block, axis, distance):
    devices = range(lax.axis_size(axis))
    route = [((i - distance) % len(devices), i) for i in devices]
    return lax.ppermute(block, axis, route)


def slot_tables(routes, experts, capacity):
    paths, tok_rows, top_count = routes.shape
    flat = routes.reshape(paths, tok_rows * top_count)
    pairs = flat.shape[1]
    earlier = jnp.arange(pairs)[None, :] < jnp.arange(pairs)[:, None]
    same = (flat[:, :, None] == flat[:, None, :]) & earlier[None]
    rank_within = jnp.sum(same.astype(jnp.int32), axis=2)
    return (flat * capacity + rank_within).reshape(paths, tok_rows, top_count)


def stage_bits(member_bits):
    core = member_bits[0]
    return [0, 1 if core == 0 else 2, 2 if core == 0 else 1]


def member_bits_of(member, group_size):
    return [member >> b & 1 for b in range(group_size.bit_length() - 1)]


def stage_route(axis_count, group_size, stage):
    route = []
    for index in range(axis_count):
        bits = member_bits_of(index % group_size, group_size)
        bit = stage_bits(bits)[stage]
        route.append((index, index ^ (1 << bit)))
    return route


def block_order(group_size):
    order = [0] * group_size
    for member in range(group_size):
        bits = member_bits_of(member, group_size)
        pos = 0
        for bit in stage_bits(bits):
            pos = pos * 2 + bits[bit]
        order[pos] = member
    return order


def own_stage_bit(index, group_size, stage):
    member = index % group_size
    core = member & 1
    if stage == 0:
        bit = 0
    elif stage == 1:
        bit = jnp.where(core == 0, 1, 2)
    else:
        bit = jnp.where(core == 0, 2, 1)
    return (member >> bit & 1).astype(jnp.int32)


def encode_rows(values, lanes):
    largest = jnp.maximum(jnp.max(jnp.abs(values), axis=1, keepdims=True), 1e-30)
    exponent = jnp.floor(jnp.log2(largest)) - 13.0
    coded = jnp.round(values * jnp.exp2(-exponent)).astype(jnp.int16)
    tail = jnp.broadcast_to(exponent.astype(jnp.int16), (values.shape[0], lanes))
    return jnp.concatenate([coded, tail], axis=1)


def decode_rows(coded, width):
    exponent = coded[:, width : width + 1].astype(jnp.float32)
    return coded[:, :width].astype(jnp.float32) * jnp.exp2(exponent)


def body(
    acts_down,
    routes_down,
    gates_down,
    grads_up,
    routes_up,
    gates_up,
    weight_in,
    weight_out,
    saved_pre,
):
    devices = lax.axis_size("expert")
    group_size = devices // EXPERTS
    levels = group_size.bit_length() - 1
    index = lax.axis_index("expert")
    model_width = acts_down.shape[2]
    share_width = model_width // group_size
    slot_count = EXPERTS * MOST
    proj_in = weight_in[0, 0]
    proj_out = weight_out[0, 0]
    hidden_units = proj_out.shape[0]
    order = block_order(group_size)

    saved_route = [
        (i, (i // group_size) * group_size + order[i % group_size]) for i in range(devices)
    ]
    saved = lax.ppermute(saved_pre[0, 0], "expert", saved_route)

    arrived = shifted(acts_down[0], "pipe", 1)
    incoming = shifted(grads_up[0], "pipe", -1)
    tokens = jnp.stack([arrived, incoming])
    routes = jnp.stack([routes_down[0], routes_up[0]])
    gates = jnp.stack([gates_down[0], gates_up[0]]).astype(jnp.float32)
    slots = slot_tables(routes, EXPERTS, MOST)
    onehot = (
        slots.transpose(0, 2, 1)[:, :, None, :]
        == jnp.arange(slot_count, dtype=jnp.int32)[None, None, :, None]
    ).astype(jnp.bfloat16)
    dispatch = jnp.sum(onehot, axis=1).reshape(2, EXPERTS, MOST, -1)
    token_parts = tokens.reshape(2, tokens.shape[1], group_size, share_width)
    sent = jnp.einsum(
        "prjt,pthc->rhpjc", dispatch, token_parts, preferred_element_type=jnp.float32
    ).astype(jnp.bfloat16)
    sent = sent.reshape(devices, 2, MOST, share_width)
    got = lax.all_to_all(sent, "expert", split_axis=0, concat_axis=0, tiled=True)
    rows_down = got[:, 0].reshape(-1, share_width)
    rows_up = got[:, 1].reshape(-1, share_width)

    def first_partial(start, count):
        part_down = lax.dynamic_slice_in_dim(rows_down, start, count, axis=0)
        part_up = lax.dynamic_slice_in_dim(rows_up, start, count, axis=0)
        pre = jnp.dot(part_down, proj_in, preferred_element_type=jnp.float32)
        grad = lax.dot_general(
            part_up, proj_out, (((1,), (1,)), ((), ())), preferred_element_type=jnp.float32
        )
        return jnp.concatenate([pre, grad], axis=1)

    half = rows_down.shape[0] // 2
    bit = own_stage_bit(index, group_size, 0)
    send_part = first_partial((1 - bit) * half, half)
    received = lax.ppermute(send_part, "expert", stage_route(devices, group_size, 0))
    current = first_partial(bit * half, half) + received
    for stage in range(1, levels):
        half = current.shape[0] // 2
        bit = own_stage_bit(index, group_size, stage)
        kept = lax.dynamic_slice_in_dim(current, bit * half, half, axis=0)
        send_part = lax.dynamic_slice_in_dim(current, (1 - bit) * half, half, axis=0)
        width = send_part.shape[1]
        received = lax.ppermute(
            encode_rows(send_part, 128), "expert", stage_route(devices, group_size, stage)
        )
        current = kept + decode_rows(received, width)

    pre_share = current[:, : 2 * hidden_units]
    hidden_grad = current[:, 2 * hidden_units :]
    hidden_share = (
        jax.nn.silu(pre_share[:, :hidden_units]) * pre_share[:, hidden_units:]
    ).astype(jnp.bfloat16)
    gate_pre = saved[:, :hidden_units].astype(jnp.float32)
    up_pre = saved[:, hidden_units:].astype(jnp.float32)
    sigmoid_gate = jax.nn.sigmoid(gate_pre)
    gate_grad = hidden_grad * up_pre * sigmoid_gate * (1.0 + gate_pre * (1.0 - sigmoid_gate))
    up_grad = hidden_grad * gate_pre * sigmoid_gate
    current = jnp.concatenate([hidden_share, gate_grad.astype(jnp.bfloat16), up_grad.astype(jnp.bfloat16)], axis=1)

    for stage in reversed(range(levels)):
        partner = lax.ppermute(current, "expert", stage_route(devices, group_size, stage))
        current = jnp.concatenate([current, partner], axis=0)
    out_down = jnp.dot(
        current[:, :hidden_units], proj_out, preferred_element_type=jnp.float32
    ).astype(jnp.bfloat16)
    out_up = lax.dot_general(
        current[:, hidden_units:], proj_in, (((1,), (1,)), ((), ())),
        preferred_element_type=jnp.float32,
    ).astype(jnp.bfloat16)
    result = jnp.stack([out_down, out_up])
    view = result.reshape((2,) + (2,) * levels + (-1, share_width))
    neighbour = index ^ 1
    for stage in reversed(range(1, levels)):
        flags = jnp.stack(
            [own_stage_bit(index, group_size, stage), own_stage_bit(neighbour, group_size, stage)]
        ).reshape((1, 2) + (1,) * (levels + 1))
        view = jnp.where(flags == 1, jnp.flip(view, axis=1 + stage), view)
    top = own_stage_bit(index, group_size, 0)
    view = jnp.where(top == 1, jnp.flip(view, axis=1), view)
    result = view.reshape(2, -1, share_width)
    result = result.reshape(2, devices, MOST, share_width).transpose(1, 0, 2, 3)
    back = lax.all_to_all(result, "expert", split_axis=0, concat_axis=0, tiled=True)
    back = back.reshape(EXPERTS, group_size, 2, MOST, share_width)
    gathered = jnp.einsum(
        "pkrjt,rhpjc->ptkhc",
        onehot.reshape(2, -1, EXPERTS, MOST, onehot.shape[-1]),
        back,
        preferred_element_type=jnp.float32,
    )
    gathered = gathered.reshape(2, tokens.shape[1], -1, model_width)
    summed = tokens.astype(jnp.float32) + jnp.sum(gates[..., None] * gathered, axis=2)
    summed = summed.astype(jnp.bfloat16)
    return (summed[0][None], summed[1][None])


def solution(mesh):
    placed = (
        P("pipe", "expert", None),
        P("pipe", "expert", None),
        P("pipe", "expert", None),
        P("pipe", "expert", None),
        P("pipe", "expert", None),
        P("pipe", "expert", None),
        P("pipe", "expert", None, None),
        P("pipe", "expert", None, None),
        P("pipe", "expert", None, None),
    )
    return jax.shard_map(
        body,
        mesh=mesh,
        in_specs=placed,
        out_specs=(P("pipe", "expert", None), P("pipe", "expert", None)),
        check_vma=False,
    )
```

```python
import numpy as np
import jax
import jax.numpy as jnp
from jax import lax
from jax.sharding import PartitionSpec as P

EXPERTS = 8
MOST = 6


def shifted(block, axis, distance):
    devices = range(lax.axis_size(axis))
    route = [((i - distance) % len(devices), i) for i in devices]
    return lax.ppermute(block, axis, route)


def slot_tables(routes, experts, capacity):
    paths, tok_rows, top_count = routes.shape
    flat = routes.reshape(paths, tok_rows * top_count)
    pairs = flat.shape[1]
    earlier = jnp.arange(pairs)[None, :] < jnp.arange(pairs)[:, None]
    same = (flat[:, :, None] == flat[:, None, :]) & earlier[None]
    rank_within = jnp.sum(same.astype(jnp.int32), axis=2)
    return (flat * capacity + rank_within).reshape(paths, tok_rows, top_count)


def stage_bits(member_bits):
    core = member_bits[0]
    return [0, 1 if core == 0 else 2, 2 if core == 0 else 1]


def member_bits_of(member, group_size):
    return [member >> b & 1 for b in range(group_size.bit_length() - 1)]


def stage_route(axis_count, group_size, stage):
    route = []
    for index in range(axis_count):
        bits = member_bits_of(index % group_size, group_size)
        bit = stage_bits(bits)[stage]
        route.append((index, index ^ (1 << bit)))
    return route


def block_order(group_size):
    order = [0] * group_size
    for member in range(group_size):
        bits = member_bits_of(member, group_size)
        pos = 0
        for bit in stage_bits(bits):
            pos = pos * 2 + bits[bit]
        order[pos] = member
    return order


def own_stage_bit(index, group_size, stage):
    member = index % group_size
    core = member & 1
    if stage == 0:
        bit = 0
    elif stage == 1:
        bit = jnp.where(core == 0, 1, 2)
    else:
        bit = jnp.where(core == 0, 2, 1)
    return (member >> bit & 1).astype(jnp.int32)


def encode_rows(values, lanes):
    largest = jnp.maximum(jnp.max(jnp.abs(values), axis=1, keepdims=True), 1e-30)
    exponent = jnp.floor(jnp.log2(largest)) - 13.0
    coded = jnp.round(values * jnp.exp2(-exponent)).astype(jnp.int16)
    tail = jnp.broadcast_to(exponent.astype(jnp.int16), (values.shape[0], lanes))
    return jnp.concatenate([coded, tail], axis=1)


def decode_rows(coded, width):
    exponent = coded[:, width : width + 1].astype(jnp.float32)
    return coded[:, :width].astype(jnp.float32) * jnp.exp2(exponent)


def body(
    acts_down,
    routes_down,
    gates_down,
    grads_up,
    routes_up,
    gates_up,
    weight_in,
    weight_out,
    saved_pre,
):
    devices = lax.axis_size("expert")
    group_size = devices // EXPERTS
    levels = group_size.bit_length() - 1
    index = lax.axis_index("expert")
    model_width = acts_down.shape[2]
    share_width = model_width // group_size
    slot_count = EXPERTS * MOST
    proj_in = weight_in[0, 0]
    proj_out = weight_out[0, 0]
    hidden_units = proj_out.shape[0]
    order = block_order(group_size)

    saved_route = [
        (i, (i // group_size) * group_size + order[i % group_size]) for i in range(devices)
    ]
    saved = lax.ppermute(saved_pre[0, 0], "expert", saved_route)

    arrived = shifted(acts_down[0], "pipe", 1)
    incoming = shifted(grads_up[0], "pipe", -1)
    tokens = jnp.stack([arrived, incoming])
    routes = jnp.stack([routes_down[0], routes_up[0]])
    gates = jnp.stack([gates_down[0], gates_up[0]]).astype(jnp.float32)
    slots = slot_tables(routes, EXPERTS, MOST)
    onehot = (
        slots.transpose(0, 2, 1)[:, :, None, :]
        == jnp.arange(slot_count, dtype=jnp.int32)[None, None, :, None]
    ).astype(jnp.bfloat16)
    dispatch = jnp.sum(onehot, axis=1).reshape(2, EXPERTS, MOST, -1)
    token_parts = tokens.reshape(2, tokens.shape[1], group_size, share_width)
    sent = jnp.einsum(
        "prjt,pthc->rhpjc", dispatch, token_parts, preferred_element_type=jnp.float32
    ).astype(jnp.bfloat16)
    sent = sent.reshape(devices, 2, MOST, share_width)
    got = lax.all_to_all(sent, "expert", split_axis=0, concat_axis=0, tiled=True)
    rows_down = got[:, 0].reshape(-1, share_width)
    rows_up = got[:, 1].reshape(-1, share_width)

    def first_partial(start, count):
        part_down = lax.dynamic_slice_in_dim(rows_down, start, count, axis=0)
        part_up = lax.dynamic_slice_in_dim(rows_up, start, count, axis=0)
        pre = jnp.dot(part_down, proj_in, preferred_element_type=jnp.float32)
        grad = lax.dot_general(
            part_up, proj_out, (((1,), (1,)), ((), ())), preferred_element_type=jnp.float32
        )
        return jnp.concatenate([pre, grad], axis=1)

    half = rows_down.shape[0] // 2
    bit = own_stage_bit(index, group_size, 0)
    send_part = first_partial((1 - bit) * half, half)
    received = lax.ppermute(send_part, "expert", stage_route(devices, group_size, 0))
    current = first_partial(bit * half, half) + received
    for stage in range(1, levels):
        half = current.shape[0] // 2
        bit = own_stage_bit(index, group_size, stage)
        kept = lax.dynamic_slice_in_dim(current, bit * half, half, axis=0)
        send_part = lax.dynamic_slice_in_dim(current, (1 - bit) * half, half, axis=0)
        width = send_part.shape[1]
        received = lax.ppermute(
            encode_rows(send_part, 128), "expert", stage_route(devices, group_size, stage)
        )
        current = kept + decode_rows(received, width)

    pre_share = current[:, : 2 * hidden_units]
    hidden_grad = current[:, 2 * hidden_units :]
    hidden_share = (
        jax.nn.silu(pre_share[:, :hidden_units]) * pre_share[:, hidden_units:]
    ).astype(jnp.bfloat16)
    gate_pre = saved[:, :hidden_units].astype(jnp.float32)
    up_pre = saved[:, hidden_units:].astype(jnp.float32)
    sigmoid_gate = jax.nn.sigmoid(gate_pre)
    gate_grad = hidden_grad * up_pre * sigmoid_gate * (1.0 + gate_pre * (1.0 - sigmoid_gate))
    up_grad = hidden_grad * gate_pre * sigmoid_gate
    current = jnp.concatenate([hidden_share, gate_grad.astype(jnp.bfloat16), up_grad.astype(jnp.bfloat16)], axis=1)

    for stage in reversed(range(1, levels)):
        partner = lax.ppermute(current, "expert", stage_route(devices, group_size, stage))
        current = jnp.concatenate([current, partner], axis=0)

    def last_matmul(block):
        out_down = jnp.dot(
            block[:, :hidden_units], proj_out, preferred_element_type=jnp.float32
        ).astype(jnp.bfloat16)
        out_up = lax.dot_general(
            block[:, hidden_units:], proj_in, (((1,), (1,)), ((), ())),
            preferred_element_type=jnp.float32,
        ).astype(jnp.bfloat16)
        return jnp.stack([out_down, out_up])

    partner = lax.ppermute(current, "expert", stage_route(devices, group_size, 0))
    own_out = last_matmul(current)
    result = jnp.concatenate([own_out, last_matmul(partner)], axis=1)
    view = result.reshape((2,) + (2,) * levels + (-1, share_width))
    neighbour = index ^ 1
    for stage in reversed(range(1, levels)):
        flags = jnp.stack(
            [own_stage_bit(index, group_size, stage), own_stage_bit(neighbour, group_size, stage)]
        ).reshape((1, 2) + (1,) * (levels + 1))
        view = jnp.where(flags == 1, jnp.flip(view, axis=1 + stage), view)
    top = own_stage_bit(index, group_size, 0)
    view = jnp.where(top == 1, jnp.flip(view, axis=1), view)
    result = view.reshape(2, -1, share_width)
    result = result.reshape(2, devices, MOST, share_width).transpose(1, 0, 2, 3)
    back = lax.all_to_all(result, "expert", split_axis=0, concat_axis=0, tiled=True)
    back = back.reshape(EXPERTS, group_size, 2, MOST, share_width)
    gathered = jnp.einsum(
        "pkrjt,rhpjc->ptkhc",
        onehot.reshape(2, -1, EXPERTS, MOST, onehot.shape[-1]),
        back,
        preferred_element_type=jnp.float32,
    )
    gathered = gathered.reshape(2, tokens.shape[1], -1, model_width)
    summed = tokens.astype(jnp.float32) + jnp.sum(gates[..., None] * gathered, axis=2)
    summed = summed.astype(jnp.bfloat16)
    return (summed[0][None], summed[1][None])


def solution(mesh):
    placed = (
        P("pipe", "expert", None),
        P("pipe", "expert", None),
        P("pipe", "expert", None),
        P("pipe", "expert", None),
        P("pipe", "expert", None),
        P("pipe", "expert", None),
        P("pipe", "expert", None, None),
        P("pipe", "expert", None, None),
        P("pipe", "expert", None, None),
    )
    return jax.shard_map(
        body,
        mesh=mesh,
        in_specs=placed,
        out_specs=(P("pipe", "expert", None), P("pipe", "expert", None)),
        check_vma=False,
    )
```

```python
import numpy as np
import jax
import jax.numpy as jnp
from jax import lax
from jax.sharding import PartitionSpec as P

EXPERTS = 8
MOST = 6


def shifted(block, axis, distance):
    devices = range(lax.axis_size(axis))
    route = [((i - distance) % len(devices), i) for i in devices]
    return lax.ppermute(block, axis, route)


def slot_tables(routes, experts, capacity):
    paths, tok_rows, top_count = routes.shape
    flat = routes.reshape(paths, tok_rows * top_count)
    pairs = flat.shape[1]
    earlier = jnp.arange(pairs)[None, :] < jnp.arange(pairs)[:, None]
    same = (flat[:, :, None] == flat[:, None, :]) & earlier[None]
    rank_within = jnp.sum(same.astype(jnp.int32), axis=2)
    return (flat * capacity + rank_within).reshape(paths, tok_rows, top_count)


def stage_bits(member_bits):
    core = member_bits[0]
    return [0, 1 if core == 0 else 2, 2 if core == 0 else 1]


def member_bits_of(member, group_size):
    return [member >> b & 1 for b in range(group_size.bit_length() - 1)]


def stage_route(axis_count, group_size, stage):
    route = []
    for index in range(axis_count):
        bits = member_bits_of(index % group_size, group_size)
        bit = stage_bits(bits)[stage]
        route.append((index, index ^ (1 << bit)))
    return route


def block_order(group_size):
    order = [0] * group_size
    for member in range(group_size):
        bits = member_bits_of(member, group_size)
        pos = 0
        for bit in stage_bits(bits):
            pos = pos * 2 + bits[bit]
        order[pos] = member
    return order


def own_stage_bit(index, group_size, stage):
    member = index % group_size
    core = member & 1
    if stage == 0:
        bit = 0
    elif stage == 1:
        bit = jnp.where(core == 0, 1, 2)
    else:
        bit = jnp.where(core == 0, 2, 1)
    return (member >> bit & 1).astype(jnp.int32)


def encode_rows(values, lanes):
    largest = jnp.maximum(jnp.max(jnp.abs(values), axis=1, keepdims=True), 1e-30)
    exponent = jnp.floor(jnp.log2(largest)) - 13.0
    coded = jnp.round(values * jnp.exp2(-exponent)).astype(jnp.int16)
    tail = jnp.broadcast_to(exponent.astype(jnp.int16), (values.shape[0], lanes))
    return jnp.concatenate([coded, tail], axis=1)


def decode_rows(coded, width):
    exponent = coded[:, width : width + 1].astype(jnp.float32)
    return coded[:, :width].astype(jnp.float32) * jnp.exp2(exponent)


def body(
    acts_down,
    routes_down,
    gates_down,
    grads_up,
    routes_up,
    gates_up,
    weight_in,
    weight_out,
    saved_pre,
):
    devices = lax.axis_size("expert")
    group_size = devices // EXPERTS
    levels = group_size.bit_length() - 1
    index = lax.axis_index("expert")
    model_width = acts_down.shape[2]
    share_width = model_width // group_size
    slot_count = EXPERTS * MOST
    proj_in = weight_in[0, 0]
    proj_out = weight_out[0, 0]
    hidden_units = proj_out.shape[0]
    order = block_order(group_size)

    saved_route = [
        (i, (i // group_size) * group_size + order[i % group_size]) for i in range(devices)
    ]
    saved = lax.ppermute(saved_pre[0, 0], "expert", saved_route)

    arrived = shifted(acts_down[0], "pipe", 1)
    incoming = shifted(grads_up[0], "pipe", -1)
    tokens = jnp.stack([arrived, incoming])
    routes = jnp.stack([routes_down[0], routes_up[0]])
    gates = jnp.stack([gates_down[0], gates_up[0]]).astype(jnp.float32)
    slots = slot_tables(routes, EXPERTS, MOST)
    onehot = (
        slots.transpose(0, 2, 1)[:, :, None, :]
        == jnp.arange(slot_count, dtype=jnp.int32)[None, None, :, None]
    ).astype(jnp.bfloat16)
    dispatch = jnp.sum(onehot, axis=1).reshape(2, EXPERTS, MOST, -1)
    token_parts = tokens.reshape(2, tokens.shape[1], group_size, share_width)
    sent = jnp.einsum(
        "prjt,pthc->rhpjc", dispatch, token_parts, preferred_element_type=jnp.float32
    ).astype(jnp.bfloat16)
    sent = sent.reshape(devices, 2, MOST, share_width)
    got = lax.all_to_all(sent, "expert", split_axis=0, concat_axis=0, tiled=True)
    rows_down = got[:, 0].reshape(-1, share_width)
    rows_up = got[:, 1].reshape(-1, share_width)

    def first_partial(start, count):
        part_down = lax.dynamic_slice_in_dim(rows_down, start, count, axis=0)
        part_up = lax.dynamic_slice_in_dim(rows_up, start, count, axis=0)
        pre = jnp.dot(part_down, proj_in, preferred_element_type=jnp.float32)
        grad = lax.dot_general(
            part_up, proj_out, (((1,), (1,)), ((), ())), preferred_element_type=jnp.float32
        )
        return jnp.concatenate([pre, grad], axis=1)

    half = rows_down.shape[0] // 2
    bit = own_stage_bit(index, group_size, 0)
    send_part = first_partial((1 - bit) * half, half)
    received = lax.ppermute(send_part, "expert", stage_route(devices, group_size, 0))
    current = first_partial(bit * half, half) + received
    for stage in range(1, levels):
        half = current.shape[0] // 2
        bit = own_stage_bit(index, group_size, stage)
        kept = lax.dynamic_slice_in_dim(current, bit * half, half, axis=0)
        send_part = lax.dynamic_slice_in_dim(current, (1 - bit) * half, half, axis=0)
        width = send_part.shape[1]
        received = lax.ppermute(
            encode_rows(send_part, 128), "expert", stage_route(devices, group_size, stage)
        )
        current = kept + decode_rows(received, width)

    pre_share = current[:, : 2 * hidden_units]
    hidden_grad = current[:, 2 * hidden_units :]
    hidden_share = (
        jax.nn.silu(pre_share[:, :hidden_units]) * pre_share[:, hidden_units:]
    ).astype(jnp.bfloat16)
    gate_pre = saved[:, :hidden_units].astype(jnp.float32)
    up_pre = saved[:, hidden_units:].astype(jnp.float32)
    sigmoid_gate = jax.nn.sigmoid(gate_pre)
    gate_grad = hidden_grad * up_pre * sigmoid_gate * (1.0 + gate_pre * (1.0 - sigmoid_gate))
    up_grad = hidden_grad * gate_pre * sigmoid_gate
    current = jnp.concatenate([hidden_share, gate_grad.astype(jnp.bfloat16), up_grad.astype(jnp.bfloat16)], axis=1)

    for stage in reversed(range(1, levels)):
        partner = lax.ppermute(current, "expert", stage_route(devices, group_size, stage))
        current = jnp.concatenate([current, partner], axis=0)

    def last_matmul(block):
        out_down = jnp.dot(
            block[:, :hidden_units], proj_out, preferred_element_type=jnp.float32
        ).astype(jnp.bfloat16)
        out_up = lax.dot_general(
            block[:, hidden_units:], proj_in, (((1,), (1,)), ((), ())),
            preferred_element_type=jnp.float32,
        ).astype(jnp.bfloat16)
        return jnp.stack([out_down, out_up])

    partner = lax.ppermute(current, "expert", stage_route(devices, group_size, 0))
    own_out = last_matmul(current)
    result = jnp.concatenate([own_out, last_matmul(partner)], axis=1)
    neighbour = index ^ 1
    flags = [
        [own_stage_bit(index, group_size, stage), own_stage_bit(neighbour, group_size, stage)]
        for stage in range(levels)
    ]
    sources = []
    for position in range(group_size):
        wanted = [position >> (levels - 1 - level) & 1 for level in range(levels)]
        first = wanted[0] ^ flags[0][0]
        source = first
        for level in range(1, levels):
            flag = jnp.where(first == 1, flags[level][1], flags[level][0])
            source = source * 2 + (wanted[level] ^ flag)
        sources.append(source)
    blocks = result.reshape(2, group_size, -1, share_width)
    result = jnp.take(blocks, jnp.stack(sources), axis=1).reshape(2, -1, share_width)
    result = result.reshape(2, devices, MOST, share_width).transpose(1, 0, 2, 3)
    back = lax.all_to_all(result, "expert", split_axis=0, concat_axis=0, tiled=True)
    back = back.reshape(EXPERTS, group_size, 2, MOST, share_width)
    gathered = jnp.einsum(
        "pkrjt,rhpjc->ptkhc",
        onehot.reshape(2, -1, EXPERTS, MOST, onehot.shape[-1]),
        back,
        preferred_element_type=jnp.float32,
    )
    gathered = gathered.reshape(2, tokens.shape[1], -1, model_width)
    summed = tokens.astype(jnp.float32) + jnp.sum(gates[..., None] * gathered, axis=2)
    summed = summed.astype(jnp.bfloat16)
    return (summed[0][None], summed[1][None])


def solution(mesh):
    placed = (
        P("pipe", "expert", None),
        P("pipe", "expert", None),
        P("pipe", "expert", None),
        P("pipe", "expert", None),
        P("pipe", "expert", None),
        P("pipe", "expert", None),
        P("pipe", "expert", None, None),
        P("pipe", "expert", None, None),
        P("pipe", "expert", None, None),
    )
    return jax.shard_map(
        body,
        mesh=mesh,
        in_specs=placed,
        out_specs=(P("pipe", "expert", None), P("pipe", "expert", None)),
        check_vma=False,
    )
```

```python
import numpy as np
import jax
import jax.numpy as jnp
from jax import lax
from jax.sharding import PartitionSpec as P

EXPERTS = 8
MOST = 6


def shifted(block, axis, distance):
    devices = range(lax.axis_size(axis))
    route = [((i - distance) % len(devices), i) for i in devices]
    return lax.ppermute(block, axis, route)


def slot_tables(routes, experts, capacity):
    paths, tok_rows, top_count = routes.shape
    flat = routes.reshape(paths, tok_rows * top_count)
    pairs = flat.shape[1]
    earlier = jnp.arange(pairs)[None, :] < jnp.arange(pairs)[:, None]
    same = (flat[:, :, None] == flat[:, None, :]) & earlier[None]
    rank_within = jnp.sum(same.astype(jnp.int32), axis=2)
    return (flat * capacity + rank_within).reshape(paths, tok_rows, top_count)


def stage_bits(member_bits):
    core = member_bits[0]
    return [0, 1 if core == 0 else 2, 2 if core == 0 else 1]


def member_bits_of(member, group_size):
    return [member >> b & 1 for b in range(group_size.bit_length() - 1)]


def stage_route(axis_count, group_size, stage):
    route = []
    for index in range(axis_count):
        bits = member_bits_of(index % group_size, group_size)
        bit = stage_bits(bits)[stage]
        route.append((index, index ^ (1 << bit)))
    return route


def block_order(group_size):
    order = [0] * group_size
    for member in range(group_size):
        bits = member_bits_of(member, group_size)
        pos = 0
        for bit in stage_bits(bits):
            pos = pos * 2 + bits[bit]
        order[pos] = member
    return order


def own_stage_bit(index, group_size, stage):
    member = index % group_size
    core = member & 1
    if stage == 0:
        bit = 0
    elif stage == 1:
        bit = jnp.where(core == 0, 1, 2)
    else:
        bit = jnp.where(core == 0, 2, 1)
    return (member >> bit & 1).astype(jnp.int32)


def encode_rows(values, lanes):
    largest = jnp.maximum(jnp.max(jnp.abs(values), axis=1, keepdims=True), 1e-30)
    exponent = jnp.floor(jnp.log2(largest)) - 13.0
    coded = jnp.round(values * jnp.exp2(-exponent)).astype(jnp.int16)
    tail = jnp.broadcast_to(exponent.astype(jnp.int16), (values.shape[0], lanes))
    return jnp.concatenate([coded, tail], axis=1)


def decode_rows(coded, width):
    exponent = coded[:, width : width + 1].astype(jnp.float32)
    return coded[:, :width].astype(jnp.float32) * jnp.exp2(exponent)


def body(
    acts_down,
    routes_down,
    gates_down,
    grads_up,
    routes_up,
    gates_up,
    weight_in,
    weight_out,
    saved_pre,
):
    devices = lax.axis_size("expert")
    group_size = devices // EXPERTS
    levels = group_size.bit_length() - 1
    index = lax.axis_index("expert")
    model_width = acts_down.shape[2]
    share_width = model_width // group_size
    slot_count = EXPERTS * MOST
    proj_in = weight_in[0, 0]
    proj_out = weight_out[0, 0]
    hidden_units = proj_out.shape[0]
    order = block_order(group_size)

    saved_route = [
        (i, (i // group_size) * group_size + order[i % group_size]) for i in range(devices)
    ]
    saved = lax.ppermute(saved_pre[0, 0], "expert", saved_route)

    arrived = shifted(acts_down[0], "pipe", 1)
    incoming = shifted(grads_up[0], "pipe", -1)
    tokens = jnp.stack([arrived, incoming])
    routes = jnp.stack([routes_down[0], routes_up[0]])
    gates = jnp.stack([gates_down[0], gates_up[0]]).astype(jnp.float32)
    slots = slot_tables(routes, EXPERTS, MOST)
    onehot = (
        slots.transpose(0, 2, 1)[:, :, None, :]
        == jnp.arange(slot_count, dtype=jnp.int32)[None, None, :, None]
    ).astype(jnp.bfloat16)
    dispatch = jnp.sum(onehot, axis=1).reshape(2, EXPERTS, MOST, -1)
    token_parts = tokens.reshape(2, tokens.shape[1], group_size, share_width)
    sent = jnp.einsum(
        "prjt,pthc->rhpjc", dispatch, token_parts, preferred_element_type=jnp.float32
    ).astype(jnp.bfloat16)
    sent = sent.reshape(devices, 2, MOST, share_width)
    saved, sent = lax.optimization_barrier((saved, sent))
    got = lax.all_to_all(sent, "expert", split_axis=0, concat_axis=0, tiled=True)
    rows_down = got[:, 0].reshape(-1, share_width)
    rows_up = got[:, 1].reshape(-1, share_width)

    def first_partial(start, count):
        part_down = lax.dynamic_slice_in_dim(rows_down, start, count, axis=0)
        part_up = lax.dynamic_slice_in_dim(rows_up, start, count, axis=0)
        pre = jnp.dot(part_down, proj_in, preferred_element_type=jnp.float32)
        grad = lax.dot_general(
            part_up, proj_out, (((1,), (1,)), ((), ())), preferred_element_type=jnp.float32
        )
        return jnp.concatenate([pre, grad], axis=1)

    half = rows_down.shape[0] // 2
    bit = own_stage_bit(index, group_size, 0)
    send_part = first_partial((1 - bit) * half, half)
    received = lax.ppermute(send_part, "expert", stage_route(devices, group_size, 0))
    current = first_partial(bit * half, half) + received
    for stage in range(1, levels):
        half = current.shape[0] // 2
        bit = own_stage_bit(index, group_size, stage)
        kept = lax.dynamic_slice_in_dim(current, bit * half, half, axis=0)
        send_part = lax.dynamic_slice_in_dim(current, (1 - bit) * half, half, axis=0)
        width = send_part.shape[1]
        received = lax.ppermute(
            encode_rows(send_part, 128), "expert", stage_route(devices, group_size, stage)
        )
        current = kept + decode_rows(received, width)

    pre_share = current[:, : 2 * hidden_units]
    hidden_grad = current[:, 2 * hidden_units :]
    hidden_share = (
        jax.nn.silu(pre_share[:, :hidden_units]) * pre_share[:, hidden_units:]
    ).astype(jnp.bfloat16)
    gate_pre = saved[:, :hidden_units].astype(jnp.float32)
    up_pre = saved[:, hidden_units:].astype(jnp.float32)
    sigmoid_gate = jax.nn.sigmoid(gate_pre)
    gate_grad = hidden_grad * up_pre * sigmoid_gate * (1.0 + gate_pre * (1.0 - sigmoid_gate))
    up_grad = hidden_grad * gate_pre * sigmoid_gate
    current = jnp.concatenate([hidden_share, gate_grad.astype(jnp.bfloat16), up_grad.astype(jnp.bfloat16)], axis=1)

    for stage in reversed(range(1, levels)):
        partner = lax.ppermute(current, "expert", stage_route(devices, group_size, stage))
        current = jnp.concatenate([current, partner], axis=0)

    def last_matmul(block):
        out_down = jnp.dot(
            block[:, :hidden_units], proj_out, preferred_element_type=jnp.float32
        ).astype(jnp.bfloat16)
        out_up = lax.dot_general(
            block[:, hidden_units:], proj_in, (((1,), (1,)), ((), ())),
            preferred_element_type=jnp.float32,
        ).astype(jnp.bfloat16)
        return jnp.stack([out_down, out_up])

    partner = lax.ppermute(current, "expert", stage_route(devices, group_size, 0))
    own_out = last_matmul(current)
    result = jnp.concatenate([own_out, last_matmul(partner)], axis=1)
    neighbour = index ^ 1
    flags = [
        [own_stage_bit(index, group_size, stage), own_stage_bit(neighbour, group_size, stage)]
        for stage in range(levels)
    ]
    sources = []
    for position in range(group_size):
        wanted = [position >> (levels - 1 - level) & 1 for level in range(levels)]
        first = wanted[0] ^ flags[0][0]
        source = first
        for level in range(1, levels):
            flag = jnp.where(first == 1, flags[level][1], flags[level][0])
            source = source * 2 + (wanted[level] ^ flag)
        sources.append(source)
    blocks = result.reshape(2, group_size, -1, share_width)
    result = jnp.take(blocks, jnp.stack(sources), axis=1).reshape(2, -1, share_width)
    result = result.reshape(2, devices, MOST, share_width).transpose(1, 0, 2, 3)
    back = lax.all_to_all(result, "expert", split_axis=0, concat_axis=0, tiled=True)
    back = back.reshape(EXPERTS, group_size, 2, MOST, share_width)
    gathered = jnp.einsum(
        "pkrjt,rhpjc->ptkhc",
        onehot.reshape(2, -1, EXPERTS, MOST, onehot.shape[-1]),
        back,
        preferred_element_type=jnp.float32,
    )
    gathered = gathered.reshape(2, tokens.shape[1], -1, model_width)
    summed = tokens.astype(jnp.float32) + jnp.sum(gates[..., None] * gathered, axis=2)
    summed = summed.astype(jnp.bfloat16)
    return (summed[0][None], summed[1][None])


def solution(mesh):
    placed = (
        P("pipe", "expert", None),
        P("pipe", "expert", None),
        P("pipe", "expert", None),
        P("pipe", "expert", None),
        P("pipe", "expert", None),
        P("pipe", "expert", None),
        P("pipe", "expert", None, None),
        P("pipe", "expert", None, None),
        P("pipe", "expert", None, None),
    )
    return jax.shard_map(
        body,
        mesh=mesh,
        in_specs=placed,
        out_specs=(P("pipe", "expert", None), P("pipe", "expert", None)),
        check_vma=False,
    )
```

```python
import numpy as np
import jax
import jax.numpy as jnp
from jax import lax
from jax.sharding import PartitionSpec as P

EXPERTS = 8
MOST = 6


def shifted(block, axis, distance):
    devices = range(lax.axis_size(axis))
    route = [((i - distance) % len(devices), i) for i in devices]
    return lax.ppermute(block, axis, route)


def slot_tables(routes, experts, capacity):
    paths, tok_rows, top_count = routes.shape
    flat = routes.reshape(paths, tok_rows * top_count)
    pairs = flat.shape[1]
    earlier = jnp.arange(pairs)[None, :] < jnp.arange(pairs)[:, None]
    same = (flat[:, :, None] == flat[:, None, :]) & earlier[None]
    rank_within = jnp.sum(same.astype(jnp.int32), axis=2)
    return (flat * capacity + rank_within).reshape(paths, tok_rows, top_count)


def stage_bits(member_bits):
    core = member_bits[0]
    return [0, 1 if core == 0 else 2, 2 if core == 0 else 1]


def member_bits_of(member, group_size):
    return [member >> b & 1 for b in range(group_size.bit_length() - 1)]


def stage_route(axis_count, group_size, stage):
    route = []
    for index in range(axis_count):
        bits = member_bits_of(index % group_size, group_size)
        bit = stage_bits(bits)[stage]
        route.append((index, index ^ (1 << bit)))
    return route


def block_order(group_size):
    order = [0] * group_size
    for member in range(group_size):
        bits = member_bits_of(member, group_size)
        pos = 0
        for bit in stage_bits(bits):
            pos = pos * 2 + bits[bit]
        order[pos] = member
    return order


def own_stage_bit(index, group_size, stage):
    member = index % group_size
    core = member & 1
    if stage == 0:
        bit = 0
    elif stage == 1:
        bit = jnp.where(core == 0, 1, 2)
    else:
        bit = jnp.where(core == 0, 2, 1)
    return (member >> bit & 1).astype(jnp.int32)


def encode_rows(values, lanes):
    rows, width = values.shape
    groups = values.reshape(rows, width // lanes, lanes)
    largest = jnp.maximum(jnp.max(jnp.abs(groups), axis=2, keepdims=True), 1e-30)
    exponent = jnp.floor(jnp.log2(largest)) - 13.0
    coded = jnp.round(groups * jnp.exp2(-exponent)).astype(jnp.int16).reshape(rows, width)
    tail = jnp.pad(exponent[:, :, 0].astype(jnp.int16), ((0, 0), (0, lanes - width // lanes)))
    return jnp.concatenate([coded, tail], axis=1)


def decode_rows(coded, width, lanes):
    rows = coded.shape[0]
    exponent = coded[:, width : width + width // lanes].astype(jnp.float32)
    groups = coded[:, :width].astype(jnp.float32).reshape(rows, width // lanes, lanes)
    return (groups * jnp.exp2(exponent)[:, :, None]).reshape(rows, width)


def body(
    acts_down,
    routes_down,
    gates_down,
    grads_up,
    routes_up,
    gates_up,
    weight_in,
    weight_out,
    saved_pre,
):
    devices = lax.axis_size("expert")
    group_size = devices // EXPERTS
    levels = group_size.bit_length() - 1
    index = lax.axis_index("expert")
    model_width = acts_down.shape[2]
    share_width = model_width // group_size
    slot_count = EXPERTS * MOST
    proj_in = weight_in[0, 0]
    proj_out = weight_out[0, 0]
    hidden_units = proj_out.shape[0]
    order = block_order(group_size)

    saved_route = [
        (i, (i // group_size) * group_size + order[i % group_size]) for i in range(devices)
    ]
    saved = lax.ppermute(saved_pre[0, 0], "expert", saved_route)

    arrived = shifted(acts_down[0], "pipe", 1)
    incoming = shifted(grads_up[0], "pipe", -1)
    tokens = jnp.stack([arrived, incoming])
    routes = jnp.stack([routes_down[0], routes_up[0]])
    gates = jnp.stack([gates_down[0], gates_up[0]]).astype(jnp.float32)
    slots = slot_tables(routes, EXPERTS, MOST)
    onehot = (
        slots.transpose(0, 2, 1)[:, :, None, :]
        == jnp.arange(slot_count, dtype=jnp.int32)[None, None, :, None]
    ).astype(jnp.bfloat16)
    dispatch = jnp.sum(onehot, axis=1).reshape(2, EXPERTS, MOST, -1)
    token_parts = tokens.reshape(2, tokens.shape[1], group_size, share_width)
    sent = jnp.einsum(
        "prjt,pthc->rhpjc", dispatch, token_parts, preferred_element_type=jnp.float32
    ).astype(jnp.bfloat16)
    sent = sent.reshape(devices, 2, MOST, share_width)
    saved, sent = lax.optimization_barrier((saved, sent))
    got = lax.all_to_all(sent, "expert", split_axis=0, concat_axis=0, tiled=True)
    rows_down = got[:, 0].reshape(-1, share_width)
    rows_up = got[:, 1].reshape(-1, share_width)

    def first_partial(start, count):
        part_down = lax.dynamic_slice_in_dim(rows_down, start, count, axis=0)
        part_up = lax.dynamic_slice_in_dim(rows_up, start, count, axis=0)
        pre = jnp.dot(part_down, proj_in, preferred_element_type=jnp.float32)
        grad = lax.dot_general(
            part_up, proj_out, (((1,), (1,)), ((), ())), preferred_element_type=jnp.float32
        )
        return jnp.concatenate([pre, grad], axis=1)

    half = rows_down.shape[0] // 2
    bit = own_stage_bit(index, group_size, 0)
    send_part = first_partial((1 - bit) * half, half)
    received = lax.ppermute(send_part, "expert", stage_route(devices, group_size, 0))
    current = first_partial(bit * half, half) + received
    for stage in range(1, levels):
        half = current.shape[0] // 2
        bit = own_stage_bit(index, group_size, stage)
        kept = lax.dynamic_slice_in_dim(current, bit * half, half, axis=0)
        send_part = lax.dynamic_slice_in_dim(current, (1 - bit) * half, half, axis=0)
        width = send_part.shape[1]
        received = lax.ppermute(
            encode_rows(send_part, 128), "expert", stage_route(devices, group_size, stage)
        )
        current = kept + decode_rows(received, width, 128)

    pre_share = current[:, : 2 * hidden_units]
    hidden_grad = current[:, 2 * hidden_units :]
    hidden_share = (
        jax.nn.silu(pre_share[:, :hidden_units]) * pre_share[:, hidden_units:]
    ).astype(jnp.bfloat16)
    gate_pre = saved[:, :hidden_units].astype(jnp.float32)
    up_pre = saved[:, hidden_units:].astype(jnp.float32)
    sigmoid_gate = jax.nn.sigmoid(gate_pre)
    gate_grad = hidden_grad * up_pre * sigmoid_gate * (1.0 + gate_pre * (1.0 - sigmoid_gate))
    up_grad = hidden_grad * gate_pre * sigmoid_gate
    current = jnp.concatenate([hidden_share, gate_grad.astype(jnp.bfloat16), up_grad.astype(jnp.bfloat16)], axis=1)

    for stage in reversed(range(1, levels)):
        partner = lax.ppermute(current, "expert", stage_route(devices, group_size, stage))
        current = jnp.concatenate([current, partner], axis=0)

    def last_matmul(block):
        out_down = jnp.dot(
            block[:, :hidden_units], proj_out, preferred_element_type=jnp.float32
        ).astype(jnp.bfloat16)
        out_up = lax.dot_general(
            block[:, hidden_units:], proj_in, (((1,), (1,)), ((), ())),
            preferred_element_type=jnp.float32,
        ).astype(jnp.bfloat16)
        return jnp.stack([out_down, out_up])

    partner = lax.ppermute(current, "expert", stage_route(devices, group_size, 0))
    own_out = last_matmul(current)
    result = jnp.concatenate([own_out, last_matmul(partner)], axis=1)
    neighbour = index ^ 1
    flags = [
        [own_stage_bit(index, group_size, stage), own_stage_bit(neighbour, group_size, stage)]
        for stage in range(levels)
    ]
    sources = []
    for position in range(group_size):
        wanted = [position >> (levels - 1 - level) & 1 for level in range(levels)]
        first = wanted[0] ^ flags[0][0]
        source = first
        for level in range(1, levels):
            flag = jnp.where(first == 1, flags[level][1], flags[level][0])
            source = source * 2 + (wanted[level] ^ flag)
        sources.append(source)
    blocks = result.reshape(2, group_size, -1, share_width)
    result = jnp.take(blocks, jnp.stack(sources), axis=1).reshape(2, -1, share_width)
    result = result.reshape(2, devices, MOST, share_width).transpose(1, 0, 2, 3)
    back = lax.all_to_all(result, "expert", split_axis=0, concat_axis=0, tiled=True)
    back = back.reshape(EXPERTS, group_size, 2, MOST, share_width)
    gathered = jnp.einsum(
        "pkrjt,rhpjc->ptkhc",
        onehot.reshape(2, -1, EXPERTS, MOST, onehot.shape[-1]),
        back,
        preferred_element_type=jnp.float32,
    )
    gathered = gathered.reshape(2, tokens.shape[1], -1, model_width)
    summed = tokens.astype(jnp.float32) + jnp.sum(gates[..., None] * gathered, axis=2)
    summed = summed.astype(jnp.bfloat16)
    return (summed[0][None], summed[1][None])


def solution(mesh):
    placed = (
        P("pipe", "expert", None),
        P("pipe", "expert", None),
        P("pipe", "expert", None),
        P("pipe", "expert", None),
        P("pipe", "expert", None),
        P("pipe", "expert", None),
        P("pipe", "expert", None, None),
        P("pipe", "expert", None, None),
        P("pipe", "expert", None, None),
    )
    return jax.shard_map(
        body,
        mesh=mesh,
        in_specs=placed,
        out_specs=(P("pipe", "expert", None), P("pipe", "expert", None)),
        check_vma=False,
    )
```

```python
import numpy as np
import jax
import jax.numpy as jnp
from jax import lax
from jax.sharding import PartitionSpec as P

EXPERTS = 8
MOST = 6


def shifted(block, axis, distance):
    devices = range(lax.axis_size(axis))
    route = [((i - distance) % len(devices), i) for i in devices]
    return lax.ppermute(block, axis, route)


def slot_tables(routes, experts, capacity):
    paths, tok_rows, top_count = routes.shape
    flat = routes.reshape(paths, tok_rows * top_count)
    pairs = flat.shape[1]
    earlier = jnp.arange(pairs)[None, :] < jnp.arange(pairs)[:, None]
    same = (flat[:, :, None] == flat[:, None, :]) & earlier[None]
    rank_within = jnp.sum(same.astype(jnp.int32), axis=2)
    return (flat * capacity + rank_within).reshape(paths, tok_rows, top_count)


def stage_bits(member_bits):
    core = member_bits[0]
    return [0, 1 if core == 0 else 2, 2 if core == 0 else 1]


def member_bits_of(member, group_size):
    return [member >> b & 1 for b in range(group_size.bit_length() - 1)]


def stage_route(axis_count, group_size, stage):
    route = []
    for index in range(axis_count):
        bits = member_bits_of(index % group_size, group_size)
        bit = stage_bits(bits)[stage]
        route.append((index, index ^ (1 << bit)))
    return route


def block_order(group_size):
    order = [0] * group_size
    for member in range(group_size):
        bits = member_bits_of(member, group_size)
        pos = 0
        for bit in stage_bits(bits):
            pos = pos * 2 + bits[bit]
        order[pos] = member
    return order


def own_stage_bit(index, group_size, stage):
    member = index % group_size
    core = member & 1
    if stage == 0:
        bit = 0
    elif stage == 1:
        bit = jnp.where(core == 0, 1, 2)
    else:
        bit = jnp.where(core == 0, 2, 1)
    return (member >> bit & 1).astype(jnp.int32)


def body(
    acts_down,
    routes_down,
    gates_down,
    grads_up,
    routes_up,
    gates_up,
    weight_in,
    weight_out,
    saved_pre,
):
    devices = lax.axis_size("expert")
    group_size = devices // EXPERTS
    levels = group_size.bit_length() - 1
    index = lax.axis_index("expert")
    model_width = acts_down.shape[2]
    share_width = model_width // group_size
    slot_count = EXPERTS * MOST
    proj_in = weight_in[0, 0]
    proj_out = weight_out[0, 0]
    hidden_units = proj_out.shape[0]
    order = block_order(group_size)

    saved_route = [
        (i, (i // group_size) * group_size + order[i % group_size]) for i in range(devices)
    ]
    saved = lax.ppermute(saved_pre[0, 0], "expert", saved_route)

    arrived = shifted(acts_down[0], "pipe", 1)
    incoming = shifted(grads_up[0], "pipe", -1)
    tokens = jnp.stack([arrived, incoming])
    routes = jnp.stack([routes_down[0], routes_up[0]])
    gates = jnp.stack([gates_down[0], gates_up[0]]).astype(jnp.float32)
    slots = slot_tables(routes, EXPERTS, MOST)
    onehot = (
        slots.transpose(0, 2, 1)[:, :, None, :]
        == jnp.arange(slot_count, dtype=jnp.int32)[None, None, :, None]
    ).astype(jnp.bfloat16)
    dispatch = jnp.sum(onehot, axis=1).reshape(2, EXPERTS, MOST, -1)
    token_parts = tokens.reshape(2, tokens.shape[1], group_size, share_width)
    sent = jnp.einsum(
        "prjt,pthc->rhpjc", dispatch, token_parts, preferred_element_type=jnp.float32
    ).astype(jnp.bfloat16)
    sent = sent.reshape(devices, 2, MOST, share_width)
    saved, sent = lax.optimization_barrier((saved, sent))
    got = lax.all_to_all(sent, "expert", split_axis=0, concat_axis=0, tiled=True)
    rows_down = got[:, 0].reshape(-1, share_width)
    rows_up = got[:, 1].reshape(-1, share_width)

    def first_partial(start, count):
        part_down = lax.dynamic_slice_in_dim(rows_down, start, count, axis=0)
        part_up = lax.dynamic_slice_in_dim(rows_up, start, count, axis=0)
        pre = jnp.dot(part_down, proj_in, preferred_element_type=jnp.float32)
        grad = lax.dot_general(
            part_up, proj_out, (((1,), (1,)), ((), ())), preferred_element_type=jnp.float32
        )
        return jnp.concatenate([pre, grad], axis=1)

    half = rows_down.shape[0] // 2
    bit = own_stage_bit(index, group_size, 0)
    send_part = first_partial((1 - bit) * half, half)
    received = lax.ppermute(send_part, "expert", stage_route(devices, group_size, 0))
    current = first_partial(bit * half, half) + received
    for stage in range(1, levels):
        half = current.shape[0] // 2
        bit = own_stage_bit(index, group_size, stage)
        kept = lax.dynamic_slice_in_dim(current, bit * half, half, axis=0)
        send_part = lax.dynamic_slice_in_dim(current, (1 - bit) * half, half, axis=0)
        received = lax.ppermute(send_part, "expert", stage_route(devices, group_size, stage))
        current = kept + received

    pre_share = current[:, : 2 * hidden_units]
    hidden_grad = current[:, 2 * hidden_units :]
    hidden_share = (
        jax.nn.silu(pre_share[:, :hidden_units]) * pre_share[:, hidden_units:]
    ).astype(jnp.bfloat16)
    gate_pre = saved[:, :hidden_units].astype(jnp.float32)
    up_pre = saved[:, hidden_units:].astype(jnp.float32)
    sigmoid_gate = jax.nn.sigmoid(gate_pre)
    gate_grad = hidden_grad * up_pre * sigmoid_gate * (1.0 + gate_pre * (1.0 - sigmoid_gate))
    up_grad = hidden_grad * gate_pre * sigmoid_gate
    current = jnp.concatenate([hidden_share, gate_grad.astype(jnp.bfloat16), up_grad.astype(jnp.bfloat16)], axis=1)

    for stage in reversed(range(1, levels)):
        partner = lax.ppermute(current, "expert", stage_route(devices, group_size, stage))
        current = jnp.concatenate([current, partner], axis=0)

    def last_matmul(block):
        out_down = jnp.dot(
            block[:, :hidden_units], proj_out, preferred_element_type=jnp.float32
        ).astype(jnp.bfloat16)
        out_up = lax.dot_general(
            block[:, hidden_units:], proj_in, (((1,), (1,)), ((), ())),
            preferred_element_type=jnp.float32,
        ).astype(jnp.bfloat16)
        return jnp.stack([out_down, out_up])

    partner = lax.ppermute(current, "expert", stage_route(devices, group_size, 0))
    own_out = last_matmul(current)
    result = jnp.concatenate([own_out, last_matmul(partner)], axis=1)
    neighbour = index ^ 1
    flags = [
        [own_stage_bit(index, group_size, stage), own_stage_bit(neighbour, group_size, stage)]
        for stage in range(levels)
    ]
    sources = []
    for position in range(group_size):
        wanted = [position >> (levels - 1 - level) & 1 for level in range(levels)]
        first = wanted[0] ^ flags[0][0]
        source = first
        for level in range(1, levels):
            flag = jnp.where(first == 1, flags[level][1], flags[level][0])
            source = source * 2 + (wanted[level] ^ flag)
        sources.append(source)
    blocks = result.reshape(2, group_size, -1, share_width)
    result = jnp.take(blocks, jnp.stack(sources), axis=1).reshape(2, -1, share_width)
    result = result.reshape(2, devices, MOST, share_width).transpose(1, 0, 2, 3)
    back = lax.all_to_all(result, "expert", split_axis=0, concat_axis=0, tiled=True)
    back = back.reshape(EXPERTS, group_size, 2, MOST, share_width)
    gathered = jnp.einsum(
        "pkrjt,rhpjc->ptkhc",
        onehot.reshape(2, -1, EXPERTS, MOST, onehot.shape[-1]),
        back,
        preferred_element_type=jnp.float32,
    )
    gathered = gathered.reshape(2, tokens.shape[1], -1, model_width)
    summed = tokens.astype(jnp.float32) + jnp.sum(gates[..., None] * gathered, axis=2)
    summed = summed.astype(jnp.bfloat16)
    return (summed[0][None], summed[1][None])


def solution(mesh):
    placed = (
        P("pipe", "expert", None),
        P("pipe", "expert", None),
        P("pipe", "expert", None),
        P("pipe", "expert", None),
        P("pipe", "expert", None),
        P("pipe", "expert", None),
        P("pipe", "expert", None, None),
        P("pipe", "expert", None, None),
        P("pipe", "expert", None, None),
    )
    return jax.shard_map(
        body,
        mesh=mesh,
        in_specs=placed,
        out_specs=(P("pipe", "expert", None), P("pipe", "expert", None)),
        check_vma=False,
    )
```

```python
import numpy as np
import jax
import jax.numpy as jnp
from jax import lax
from jax.sharding import PartitionSpec as P

EXPERTS = 8
MOST = 6


def shifted(block, axis, distance):
    devices = range(lax.axis_size(axis))
    route = [((i - distance) % len(devices), i) for i in devices]
    return lax.ppermute(block, axis, route)


def slot_tables(routes, experts, capacity):
    paths, tok_rows, top_count = routes.shape
    flat = routes.reshape(paths, tok_rows * top_count)
    pairs = flat.shape[1]
    earlier = jnp.arange(pairs)[None, :] < jnp.arange(pairs)[:, None]
    same = (flat[:, :, None] == flat[:, None, :]) & earlier[None]
    rank_within = jnp.sum(same.astype(jnp.int32), axis=2)
    return (flat * capacity + rank_within).reshape(paths, tok_rows, top_count)


def stage_bits(member_bits):
    core = member_bits[0]
    return [0, 1 if core == 0 else 2, 2 if core == 0 else 1]


def member_bits_of(member, group_size):
    return [member >> b & 1 for b in range(group_size.bit_length() - 1)]


def stage_route(axis_count, group_size, stage):
    route = []
    for index in range(axis_count):
        bits = member_bits_of(index % group_size, group_size)
        bit = stage_bits(bits)[stage]
        route.append((index, index ^ (1 << bit)))
    return route


def block_order(group_size):
    order = [0] * group_size
    for member in range(group_size):
        bits = member_bits_of(member, group_size)
        pos = 0
        for bit in stage_bits(bits):
            pos = pos * 2 + bits[bit]
        order[pos] = member
    return order


def own_stage_bit(index, group_size, stage):
    member = index % group_size
    core = member & 1
    if stage == 0:
        bit = 0
    elif stage == 1:
        bit = jnp.where(core == 0, 1, 2)
    else:
        bit = jnp.where(core == 0, 2, 1)
    return (member >> bit & 1).astype(jnp.int32)


def body(
    acts_down,
    routes_down,
    gates_down,
    grads_up,
    routes_up,
    gates_up,
    weight_in,
    weight_out,
    saved_pre,
):
    devices = lax.axis_size("expert")
    group_size = devices // EXPERTS
    levels = group_size.bit_length() - 1
    index = lax.axis_index("expert")
    model_width = acts_down.shape[2]
    share_width = model_width // group_size
    slot_count = EXPERTS * MOST
    proj_in = weight_in[0, 0]
    proj_out = weight_out[0, 0]
    hidden_units = proj_out.shape[0]
    order = block_order(group_size)

    saved_route = [
        (i, (i // group_size) * group_size + order[i % group_size]) for i in range(devices)
    ]
    saved = lax.ppermute(saved_pre[0, 0], "expert", saved_route)

    arrived = shifted(acts_down[0], "pipe", 1)
    incoming = shifted(grads_up[0], "pipe", -1)
    tokens = jnp.stack([arrived, incoming])
    routes = jnp.stack([routes_down[0], routes_up[0]])
    gates = jnp.stack([gates_down[0], gates_up[0]]).astype(jnp.float32)
    slots = slot_tables(routes, EXPERTS, MOST)
    onehot = (
        slots.transpose(0, 2, 1)[:, :, None, :]
        == jnp.arange(slot_count, dtype=jnp.int32)[None, None, :, None]
    ).astype(jnp.bfloat16)
    dispatch = jnp.sum(onehot, axis=1).reshape(2, EXPERTS, MOST, -1)
    token_parts = tokens.reshape(2, tokens.shape[1], group_size, share_width)
    sent = jnp.einsum(
        "prjt,pthc->rhpjc", dispatch, token_parts, preferred_element_type=jnp.float32
    ).astype(jnp.bfloat16)
    sent = sent.reshape(devices, 2, MOST, share_width)
    saved, sent = lax.optimization_barrier((saved, sent))
    got = lax.all_to_all(sent, "expert", split_axis=0, concat_axis=0, tiled=True)
    rows_down = got[:, 0].reshape(-1, share_width)
    rows_up = got[:, 1].reshape(-1, share_width)

    both_proj = jnp.concatenate(
        [
            jnp.concatenate([proj_in, jnp.zeros((share_width, hidden_units), proj_in.dtype)], axis=1),
            jnp.concatenate([jnp.zeros((share_width, 2 * hidden_units), proj_out.dtype), proj_out.T], axis=1),
        ],
        axis=0,
    )
    both_rows = jnp.concatenate([rows_down, rows_up], axis=1)

    def first_partial(start, count):
        part = lax.dynamic_slice_in_dim(both_rows, start, count, axis=0)
        return jnp.dot(part, both_proj, preferred_element_type=jnp.float32)

    half = rows_down.shape[0] // 2
    bit = own_stage_bit(index, group_size, 0)
    send_part = first_partial((1 - bit) * half, half)
    received = lax.ppermute(send_part, "expert", stage_route(devices, group_size, 0))
    current = first_partial(bit * half, half) + received
    for stage in range(1, levels):
        half = current.shape[0] // 2
        bit = own_stage_bit(index, group_size, stage)
        kept = lax.dynamic_slice_in_dim(current, bit * half, half, axis=0)
        send_part = lax.dynamic_slice_in_dim(current, (1 - bit) * half, half, axis=0)
        received = lax.ppermute(send_part, "expert", stage_route(devices, group_size, stage))
        current = kept + received

    pre_share = current[:, : 2 * hidden_units]
    hidden_grad = current[:, 2 * hidden_units :]
    hidden_share = (
        jax.nn.silu(pre_share[:, :hidden_units]) * pre_share[:, hidden_units:]
    ).astype(jnp.bfloat16)
    gate_pre = saved[:, :hidden_units].astype(jnp.float32)
    up_pre = saved[:, hidden_units:].astype(jnp.float32)
    sigmoid_gate = jax.nn.sigmoid(gate_pre)
    gate_grad = hidden_grad * up_pre * sigmoid_gate * (1.0 + gate_pre * (1.0 - sigmoid_gate))
    up_grad = hidden_grad * gate_pre * sigmoid_gate
    current = jnp.concatenate([hidden_share, gate_grad.astype(jnp.bfloat16), up_grad.astype(jnp.bfloat16)], axis=1)

    for stage in reversed(range(1, levels)):
        partner = lax.ppermute(current, "expert", stage_route(devices, group_size, stage))
        current = jnp.concatenate([current, partner], axis=0)

    def last_matmul(block):
        out_down = jnp.dot(
            block[:, :hidden_units], proj_out, preferred_element_type=jnp.float32
        ).astype(jnp.bfloat16)
        out_up = lax.dot_general(
            block[:, hidden_units:], proj_in, (((1,), (1,)), ((), ())),
            preferred_element_type=jnp.float32,
        ).astype(jnp.bfloat16)
        return jnp.stack([out_down, out_up])

    partner = lax.ppermute(current, "expert", stage_route(devices, group_size, 0))
    own_out = last_matmul(current)
    result = jnp.concatenate([own_out, last_matmul(partner)], axis=1)
    neighbour = index ^ 1
    flags = [
        [own_stage_bit(index, group_size, stage), own_stage_bit(neighbour, group_size, stage)]
        for stage in range(levels)
    ]
    sources = []
    for position in range(group_size):
        wanted = [position >> (levels - 1 - level) & 1 for level in range(levels)]
        first = wanted[0] ^ flags[0][0]
        source = first
        for level in range(1, levels):
            flag = jnp.where(first == 1, flags[level][1], flags[level][0])
            source = source * 2 + (wanted[level] ^ flag)
        sources.append(source)
    blocks = result.reshape(2, group_size, -1, share_width)
    result = jnp.take(blocks, jnp.stack(sources), axis=1).reshape(2, -1, share_width)
    result = result.reshape(2, devices, MOST, share_width).transpose(1, 0, 2, 3)
    back = lax.all_to_all(result, "expert", split_axis=0, concat_axis=0, tiled=True)
    back = back.reshape(EXPERTS, group_size, 2, MOST, share_width)
    gathered = jnp.einsum(
        "pkrjt,rhpjc->ptkhc",
        onehot.reshape(2, -1, EXPERTS, MOST, onehot.shape[-1]),
        back,
        preferred_element_type=jnp.float32,
    )
    gathered = gathered.reshape(2, tokens.shape[1], -1, model_width)
    summed = tokens.astype(jnp.float32) + jnp.sum(gates[..., None] * gathered, axis=2)
    summed = summed.astype(jnp.bfloat16)
    return (summed[0][None], summed[1][None])


def solution(mesh):
    placed = (
        P("pipe", "expert", None),
        P("pipe", "expert", None),
        P("pipe", "expert", None),
        P("pipe", "expert", None),
        P("pipe", "expert", None),
        P("pipe", "expert", None),
        P("pipe", "expert", None, None),
        P("pipe", "expert", None, None),
        P("pipe", "expert", None, None),
    )
    return jax.shard_map(
        body,
        mesh=mesh,
        in_specs=placed,
        out_specs=(P("pipe", "expert", None), P("pipe", "expert", None)),
        check_vma=False,
    )
```

```python
import numpy as np
import jax
import jax.numpy as jnp
from jax import lax
from jax.sharding import PartitionSpec as P

EXPERTS = 8
MOST = 6


def shifted(block, axis, distance):
    devices = range(lax.axis_size(axis))
    route = [((i - distance) % len(devices), i) for i in devices]
    return lax.ppermute(block, axis, route)


def slot_tables(routes, experts, capacity):
    paths, tok_rows, top_count = routes.shape
    flat = routes.reshape(paths, tok_rows * top_count)
    pairs = flat.shape[1]
    earlier = jnp.arange(pairs)[None, :] < jnp.arange(pairs)[:, None]
    same = (flat[:, :, None] == flat[:, None, :]) & earlier[None]
    rank_within = jnp.sum(same.astype(jnp.int32), axis=2)
    return (flat * capacity + rank_within).reshape(paths, tok_rows, top_count)


def stage_bits(member_bits):
    core = member_bits[0]
    return [0, 1 if core == 0 else 2, 2 if core == 0 else 1]


def member_bits_of(member, group_size):
    return [member >> b & 1 for b in range(group_size.bit_length() - 1)]


def stage_route(axis_count, group_size, stage):
    route = []
    for index in range(axis_count):
        bits = member_bits_of(index % group_size, group_size)
        bit = stage_bits(bits)[stage]
        route.append((index, index ^ (1 << bit)))
    return route


def block_order(group_size):
    order = [0] * group_size
    for member in range(group_size):
        bits = member_bits_of(member, group_size)
        pos = 0
        for bit in stage_bits(bits):
            pos = pos * 2 + bits[bit]
        order[pos] = member
    return order


def own_stage_bit(index, group_size, stage):
    member = index % group_size
    core = member & 1
    if stage == 0:
        bit = 0
    elif stage == 1:
        bit = jnp.where(core == 0, 1, 2)
    else:
        bit = jnp.where(core == 0, 2, 1)
    return (member >> bit & 1).astype(jnp.int32)


def body(
    acts_down,
    routes_down,
    gates_down,
    grads_up,
    routes_up,
    gates_up,
    weight_in,
    weight_out,
    saved_pre,
):
    devices = lax.axis_size("expert")
    group_size = devices // EXPERTS
    levels = group_size.bit_length() - 1
    index = lax.axis_index("expert")
    model_width = acts_down.shape[2]
    share_width = model_width // group_size
    slot_count = EXPERTS * MOST
    proj_in = weight_in[0, 0]
    proj_out = weight_out[0, 0]
    hidden_units = proj_out.shape[0]
    order = block_order(group_size)

    saved_route = [
        (i, (i // group_size) * group_size + order[i % group_size]) for i in range(devices)
    ]
    saved = lax.ppermute(saved_pre[0, 0], "expert", saved_route)

    arrived = shifted(acts_down[0], "pipe", 1)
    incoming = shifted(grads_up[0], "pipe", -1)
    tokens = jnp.stack([arrived, incoming])
    routes = jnp.stack([routes_down[0], routes_up[0]])
    gates = jnp.stack([gates_down[0], gates_up[0]]).astype(jnp.float32)
    slots = slot_tables(routes, EXPERTS, MOST)
    onehot = (
        slots.transpose(0, 2, 1)[:, :, None, :]
        == jnp.arange(slot_count, dtype=jnp.int32)[None, None, :, None]
    ).astype(jnp.bfloat16)
    dispatch = jnp.sum(onehot, axis=1).reshape(2, EXPERTS, MOST, -1)
    token_parts = tokens.reshape(2, tokens.shape[1], group_size, share_width)
    sent = jnp.einsum(
        "prjt,pthc->rhpjc", dispatch, token_parts, preferred_element_type=jnp.float32
    ).astype(jnp.bfloat16)
    sent = sent.reshape(devices, 2, MOST, share_width)
    saved, sent = lax.optimization_barrier((saved, sent))
    got = lax.all_to_all(sent, "expert", split_axis=0, concat_axis=0, tiled=True)
    rows_down = got[:, 0].reshape(-1, share_width)
    rows_up = got[:, 1].reshape(-1, share_width)

    both_proj = jnp.concatenate(
        [
            jnp.concatenate([proj_in, jnp.zeros((share_width, hidden_units), proj_in.dtype)], axis=1),
            jnp.concatenate([jnp.zeros((share_width, 2 * hidden_units), proj_out.dtype), proj_out.T], axis=1),
        ],
        axis=0,
    )
    both_rows = jnp.concatenate([rows_down, rows_up], axis=1)

    def first_partial(start, count):
        part = lax.dynamic_slice_in_dim(both_rows, start, count, axis=0)
        return jnp.dot(part, both_proj, preferred_element_type=jnp.float32)

    half = rows_down.shape[0] // 2
    bit = own_stage_bit(index, group_size, 0)
    send_part = first_partial((1 - bit) * half, half)
    received = lax.ppermute(send_part, "expert", stage_route(devices, group_size, 0))
    current = first_partial(bit * half, half) + received
    for stage in range(1, levels):
        half = current.shape[0] // 2
        bit = own_stage_bit(index, group_size, stage)
        kept = lax.dynamic_slice_in_dim(current, bit * half, half, axis=0)
        send_part = lax.dynamic_slice_in_dim(current, (1 - bit) * half, half, axis=0)
        received = lax.ppermute(send_part, "expert", stage_route(devices, group_size, stage))
        current = kept + received

    pre_share = current[:, : 2 * hidden_units]
    hidden_grad = current[:, 2 * hidden_units :]
    hidden_share = (
        jax.nn.silu(pre_share[:, :hidden_units]) * pre_share[:, hidden_units:]
    ).astype(jnp.bfloat16)
    gate_pre = saved[:, :hidden_units].astype(jnp.float32)
    up_pre = saved[:, hidden_units:].astype(jnp.float32)
    sigmoid_gate = jax.nn.sigmoid(gate_pre)
    gate_grad = hidden_grad * up_pre * sigmoid_gate * (1.0 + gate_pre * (1.0 - sigmoid_gate))
    up_grad = hidden_grad * gate_pre * sigmoid_gate
    current = jnp.concatenate([hidden_share, gate_grad.astype(jnp.bfloat16), up_grad.astype(jnp.bfloat16)], axis=1)

    for stage in reversed(range(1, levels)):
        partner = lax.ppermute(current, "expert", stage_route(devices, group_size, stage))
        current = jnp.concatenate([current, partner], axis=0)

    last_proj = jnp.concatenate(
        [
            jnp.concatenate([proj_out, jnp.zeros((hidden_units, share_width), proj_out.dtype)], axis=1),
            jnp.concatenate([jnp.zeros((2 * hidden_units, share_width), proj_in.dtype), proj_in.T], axis=1),
        ],
        axis=0,
    )

    def last_matmul(block):
        both = jnp.dot(block, last_proj, preferred_element_type=jnp.float32).astype(jnp.bfloat16)
        return jnp.stack([both[:, :share_width], both[:, share_width:]])

    partner = lax.ppermute(current, "expert", stage_route(devices, group_size, 0))
    own_out = last_matmul(current)
    result = jnp.concatenate([own_out, last_matmul(partner)], axis=1)
    neighbour = index ^ 1
    flags = [
        [own_stage_bit(index, group_size, stage), own_stage_bit(neighbour, group_size, stage)]
        for stage in range(levels)
    ]
    sources = []
    for position in range(group_size):
        wanted = [position >> (levels - 1 - level) & 1 for level in range(levels)]
        first = wanted[0] ^ flags[0][0]
        source = first
        for level in range(1, levels):
            flag = jnp.where(first == 1, flags[level][1], flags[level][0])
            source = source * 2 + (wanted[level] ^ flag)
        sources.append(source)
    blocks = result.reshape(2, group_size, -1, share_width)
    result = jnp.take(blocks, jnp.stack(sources), axis=1).reshape(2, -1, share_width)
    result = result.reshape(2, devices, MOST, share_width).transpose(1, 0, 2, 3)
    back = lax.all_to_all(result, "expert", split_axis=0, concat_axis=0, tiled=True)
    back = back.reshape(EXPERTS, group_size, 2, MOST, share_width)
    gathered = jnp.einsum(
        "pkrjt,rhpjc->ptkhc",
        onehot.reshape(2, -1, EXPERTS, MOST, onehot.shape[-1]),
        back,
        preferred_element_type=jnp.float32,
    )
    gathered = gathered.reshape(2, tokens.shape[1], -1, model_width)
    summed = tokens.astype(jnp.float32) + jnp.sum(gates[..., None] * gathered, axis=2)
    summed = summed.astype(jnp.bfloat16)
    return (summed[0][None], summed[1][None])


def solution(mesh):
    placed = (
        P("pipe", "expert", None),
        P("pipe", "expert", None),
        P("pipe", "expert", None),
        P("pipe", "expert", None),
        P("pipe", "expert", None),
        P("pipe", "expert", None),
        P("pipe", "expert", None, None),
        P("pipe", "expert", None, None),
        P("pipe", "expert", None, None),
    )
    return jax.shard_map(
        body,
        mesh=mesh,
        in_specs=placed,
        out_specs=(P("pipe", "expert", None), P("pipe", "expert", None)),
        check_vma=False,
    )
```

```python
import numpy as np
import jax
import jax.numpy as jnp
from jax import lax
from jax.sharding import PartitionSpec as P

EXPERTS = 8
MOST = 6


def shifted(block, axis, distance):
    devices = range(lax.axis_size(axis))
    route = [((i - distance) % len(devices), i) for i in devices]
    return lax.ppermute(block, axis, route)


def slot_tables(routes, experts, capacity):
    paths, tok_rows, top_count = routes.shape
    flat = routes.reshape(paths, tok_rows * top_count)
    pairs = flat.shape[1]
    earlier = jnp.arange(pairs)[None, :] < jnp.arange(pairs)[:, None]
    same = (flat[:, :, None] == flat[:, None, :]) & earlier[None]
    rank_within = jnp.sum(same.astype(jnp.int32), axis=2)
    return (flat * capacity + rank_within).reshape(paths, tok_rows, top_count)


def stage_bits(member_bits):
    core = member_bits[0]
    return [0, 1 if core == 0 else 2, 2 if core == 0 else 1]


def member_bits_of(member, group_size):
    return [member >> b & 1 for b in range(group_size.bit_length() - 1)]


def stage_route(axis_count, group_size, stage):
    route = []
    for index in range(axis_count):
        bits = member_bits_of(index % group_size, group_size)
        bit = stage_bits(bits)[stage]
        route.append((index, index ^ (1 << bit)))
    return route


def block_order(group_size):
    order = [0] * group_size
    for member in range(group_size):
        bits = member_bits_of(member, group_size)
        pos = 0
        for bit in stage_bits(bits):
            pos = pos * 2 + bits[bit]
        order[pos] = member
    return order


def own_stage_bit(index, group_size, stage):
    member = index % group_size
    core = member & 1
    if stage == 0:
        bit = 0
    elif stage == 1:
        bit = jnp.where(core == 0, 1, 2)
    else:
        bit = jnp.where(core == 0, 2, 1)
    return (member >> bit & 1).astype(jnp.int32)


def body(
    acts_down,
    routes_down,
    gates_down,
    grads_up,
    routes_up,
    gates_up,
    weight_in,
    weight_out,
    saved_pre,
):
    devices = lax.axis_size("expert")
    group_size = devices // EXPERTS
    levels = group_size.bit_length() - 1
    index = lax.axis_index("expert")
    model_width = acts_down.shape[2]
    share_width = model_width // group_size
    slot_count = EXPERTS * MOST
    proj_in = weight_in[0, 0]
    proj_out = weight_out[0, 0]
    hidden_units = proj_out.shape[0]
    order = block_order(group_size)

    saved_route = [
        (i, (i // group_size) * group_size + order[i % group_size]) for i in range(devices)
    ]
    saved = lax.ppermute(saved_pre[0, 0], "expert", saved_route)

    arrived = shifted(acts_down[0], "pipe", 1)
    incoming = shifted(grads_up[0], "pipe", -1)
    tokens = jnp.stack([arrived, incoming])
    routes = jnp.stack([routes_down[0], routes_up[0]])
    gates = jnp.stack([gates_down[0], gates_up[0]]).astype(jnp.float32)
    slots = slot_tables(routes, EXPERTS, MOST)
    onehot = (
        slots.transpose(0, 2, 1)[:, :, None, :]
        == jnp.arange(slot_count, dtype=jnp.int32)[None, None, :, None]
    ).astype(jnp.bfloat16)
    dispatch = jnp.sum(onehot, axis=1).reshape(2, EXPERTS, MOST, -1)
    token_parts = tokens.reshape(2, tokens.shape[1], group_size, share_width)
    sent = jnp.einsum(
        "prjt,pthc->rhpjc", dispatch, token_parts, preferred_element_type=jnp.float32
    ).astype(jnp.bfloat16)
    sent = sent.reshape(devices, 2, MOST, share_width)
    saved, sent = lax.optimization_barrier((saved, sent))
    got = lax.all_to_all(sent, "expert", split_axis=0, concat_axis=0, tiled=True)
    rows_down = got[:, 0].reshape(-1, share_width)
    rows_up = got[:, 1].reshape(-1, share_width)

    both_proj = jnp.concatenate(
        [
            jnp.concatenate([proj_in, jnp.zeros((share_width, hidden_units), proj_in.dtype)], axis=1),
            jnp.concatenate([jnp.zeros((share_width, 2 * hidden_units), proj_out.dtype), proj_out.T], axis=1),
        ],
        axis=0,
    )
    both_rows = jnp.concatenate([rows_down, rows_up], axis=1)

    def first_partial(start, count):
        part = lax.dynamic_slice_in_dim(both_rows, start, count, axis=0)
        return jnp.dot(part, both_proj, preferred_element_type=jnp.float32)

    half = rows_down.shape[0] // 2
    bit = own_stage_bit(index, group_size, 0)
    send_part = first_partial((1 - bit) * half, half)
    received = lax.ppermute(send_part, "expert", stage_route(devices, group_size, 0))
    current = lax.optimization_barrier(first_partial(bit * half, half)) + received
    for stage in range(1, levels):
        half = current.shape[0] // 2
        bit = own_stage_bit(index, group_size, stage)
        kept = lax.dynamic_slice_in_dim(current, bit * half, half, axis=0)
        send_part = lax.dynamic_slice_in_dim(current, (1 - bit) * half, half, axis=0)
        received = lax.ppermute(send_part, "expert", stage_route(devices, group_size, stage))
        current = kept + received

    pre_share = current[:, : 2 * hidden_units]
    hidden_grad = current[:, 2 * hidden_units :]
    hidden_share = (
        jax.nn.silu(pre_share[:, :hidden_units]) * pre_share[:, hidden_units:]
    ).astype(jnp.bfloat16)
    gate_pre = saved[:, :hidden_units].astype(jnp.float32)
    up_pre = saved[:, hidden_units:].astype(jnp.float32)
    sigmoid_gate = jax.nn.sigmoid(gate_pre)
    gate_grad = hidden_grad * up_pre * sigmoid_gate * (1.0 + gate_pre * (1.0 - sigmoid_gate))
    up_grad = hidden_grad * gate_pre * sigmoid_gate
    current = jnp.concatenate([hidden_share, gate_grad.astype(jnp.bfloat16), up_grad.astype(jnp.bfloat16)], axis=1)

    for stage in reversed(range(1, levels)):
        partner = lax.ppermute(current, "expert", stage_route(devices, group_size, stage))
        current = jnp.concatenate([current, partner], axis=0)

    def last_matmul(block):
        out_down = jnp.dot(
            block[:, :hidden_units], proj_out, preferred_element_type=jnp.float32
        ).astype(jnp.bfloat16)
        out_up = lax.dot_general(
            block[:, hidden_units:], proj_in, (((1,), (1,)), ((), ())),
            preferred_element_type=jnp.float32,
        ).astype(jnp.bfloat16)
        return jnp.stack([out_down, out_up])

    partner = lax.ppermute(current, "expert", stage_route(devices, group_size, 0))
    own_out = last_matmul(current)
    result = jnp.concatenate([own_out, last_matmul(partner)], axis=1)
    neighbour = index ^ 1
    flags = [
        [own_stage_bit(index, group_size, stage), own_stage_bit(neighbour, group_size, stage)]
        for stage in range(levels)
    ]
    sources = []
    for position in range(group_size):
        wanted = [position >> (levels - 1 - level) & 1 for level in range(levels)]
        first = wanted[0] ^ flags[0][0]
        source = first
        for level in range(1, levels):
            flag = jnp.where(first == 1, flags[level][1], flags[level][0])
            source = source * 2 + (wanted[level] ^ flag)
        sources.append(source)
    blocks = result.reshape(2, group_size, -1, share_width)
    result = jnp.take(blocks, jnp.stack(sources), axis=1).reshape(2, -1, share_width)
    result = result.reshape(2, devices, MOST, share_width).transpose(1, 0, 2, 3)
    back = lax.all_to_all(result, "expert", split_axis=0, concat_axis=0, tiled=True)
    back = back.reshape(EXPERTS, group_size, 2, MOST, share_width)
    gathered = jnp.einsum(
        "pkrjt,rhpjc->ptkhc",
        onehot.reshape(2, -1, EXPERTS, MOST, onehot.shape[-1]),
        back,
        preferred_element_type=jnp.float32,
    )
    gathered = gathered.reshape(2, tokens.shape[1], -1, model_width)
    summed = tokens.astype(jnp.float32) + jnp.sum(gates[..., None] * gathered, axis=2)
    summed = summed.astype(jnp.bfloat16)
    return (summed[0][None], summed[1][None])


def solution(mesh):
    placed = (
        P("pipe", "expert", None),
        P("pipe", "expert", None),
        P("pipe", "expert", None),
        P("pipe", "expert", None),
        P("pipe", "expert", None),
        P("pipe", "expert", None),
        P("pipe", "expert", None, None),
        P("pipe", "expert", None, None),
        P("pipe", "expert", None, None),
    )
    return jax.shard_map(
        body,
        mesh=mesh,
        in_specs=placed,
        out_specs=(P("pipe", "expert", None), P("pipe", "expert", None)),
        check_vma=False,
    )
```

```python
import numpy as np
import jax
import jax.numpy as jnp
from jax import lax
from jax.sharding import PartitionSpec as P

EXPERTS = 8
MOST = 6


def shifted(block, axis, distance):
    devices = range(lax.axis_size(axis))
    route = [((i - distance) % len(devices), i) for i in devices]
    return lax.ppermute(block, axis, route)


def slot_tables(routes, experts, capacity):
    paths, tok_rows, top_count = routes.shape
    flat = routes.reshape(paths, tok_rows * top_count)
    pairs = flat.shape[1]
    earlier = jnp.arange(pairs)[None, :] < jnp.arange(pairs)[:, None]
    same = (flat[:, :, None] == flat[:, None, :]) & earlier[None]
    rank_within = jnp.sum(same.astype(jnp.int32), axis=2)
    return (flat * capacity + rank_within).reshape(paths, tok_rows, top_count)


def stage_bits(member_bits):
    core = member_bits[0]
    return [0, 1 if core == 0 else 2, 2 if core == 0 else 1]


def member_bits_of(member, group_size):
    return [member >> b & 1 for b in range(group_size.bit_length() - 1)]


def stage_route(axis_count, group_size, stage):
    route = []
    for index in range(axis_count):
        bits = member_bits_of(index % group_size, group_size)
        bit = stage_bits(bits)[stage]
        route.append((index, index ^ (1 << bit)))
    return route


def block_order(group_size):
    order = [0] * group_size
    for member in range(group_size):
        bits = member_bits_of(member, group_size)
        pos = 0
        for bit in stage_bits(bits):
            pos = pos * 2 + bits[bit]
        order[pos] = member
    return order


def own_stage_bit(index, group_size, stage):
    member = index % group_size
    core = member & 1
    if stage == 0:
        bit = 0
    elif stage == 1:
        bit = jnp.where(core == 0, 1, 2)
    else:
        bit = jnp.where(core == 0, 2, 1)
    return (member >> bit & 1).astype(jnp.int32)


def body(
    acts_down,
    routes_down,
    gates_down,
    grads_up,
    routes_up,
    gates_up,
    weight_in,
    weight_out,
    saved_pre,
):
    devices = lax.axis_size("expert")
    group_size = devices // EXPERTS
    levels = group_size.bit_length() - 1
    index = lax.axis_index("expert")
    model_width = acts_down.shape[2]
    share_width = model_width // group_size
    slot_count = EXPERTS * MOST
    proj_in = weight_in[0, 0]
    proj_out = weight_out[0, 0]
    hidden_units = proj_out.shape[0]
    order = block_order(group_size)

    saved_route = [
        (i, (i // group_size) * group_size + order[i % group_size]) for i in range(devices)
    ]
    saved = lax.ppermute(saved_pre[0, 0], "expert", saved_route)

    arrived = shifted(acts_down[0], "pipe", 1)
    incoming = shifted(grads_up[0], "pipe", -1)
    tokens = jnp.stack([arrived, incoming])
    routes = jnp.stack([routes_down[0], routes_up[0]])
    gates = jnp.stack([gates_down[0], gates_up[0]]).astype(jnp.float32)
    slots = slot_tables(routes, EXPERTS, MOST)
    onehot = (
        slots.transpose(0, 2, 1)[:, :, None, :]
        == jnp.arange(slot_count, dtype=jnp.int32)[None, None, :, None]
    ).astype(jnp.bfloat16)
    dispatch = jnp.sum(onehot, axis=1).reshape(2, EXPERTS, MOST, -1)
    token_parts = tokens.reshape(2, tokens.shape[1], group_size, share_width)
    sent = jnp.einsum(
        "prjt,pthc->rhpjc", dispatch, token_parts, preferred_element_type=jnp.float32
    ).astype(jnp.bfloat16)
    sent = sent.reshape(devices, 2, MOST, share_width)
    saved, sent = lax.optimization_barrier((saved, sent))
    got = lax.all_to_all(sent, "expert", split_axis=0, concat_axis=0, tiled=True)
    rows_down = got[:, 0].reshape(-1, share_width)
    rows_up = got[:, 1].reshape(-1, share_width)

    both_proj = jnp.concatenate(
        [
            jnp.concatenate([proj_in, jnp.zeros((share_width, hidden_units), proj_in.dtype)], axis=1),
            jnp.concatenate([jnp.zeros((share_width, 2 * hidden_units), proj_out.dtype), proj_out.T], axis=1),
        ],
        axis=0,
    )
    both_rows = jnp.concatenate([rows_down, rows_up], axis=1)

    def first_partial(start, count):
        part = lax.dynamic_slice_in_dim(both_rows, start, count, axis=0)
        return jnp.dot(part, both_proj, preferred_element_type=jnp.float32)

    half = rows_down.shape[0] // 2
    bit = own_stage_bit(index, group_size, 0)
    sent_down = lax.dynamic_slice_in_dim(rows_down, (1 - bit) * half, half, axis=0)
    sent_up = lax.dynamic_slice_in_dim(rows_up, (1 - bit) * half, half, axis=0)
    send_part = jnp.concatenate(
        [
            jnp.dot(sent_down, proj_in, preferred_element_type=jnp.float32),
            lax.dot_general(
                sent_up, proj_out, (((1,), (1,)), ((), ())), preferred_element_type=jnp.float32
            ),
        ],
        axis=1,
    )
    received = lax.ppermute(send_part, "expert", stage_route(devices, group_size, 0))
    current = lax.optimization_barrier(first_partial(bit * half, half)) + received
    for stage in range(1, levels):
        half = current.shape[0] // 2
        bit = own_stage_bit(index, group_size, stage)
        kept = lax.dynamic_slice_in_dim(current, bit * half, half, axis=0)
        send_part = lax.dynamic_slice_in_dim(current, (1 - bit) * half, half, axis=0)
        received = lax.ppermute(send_part, "expert", stage_route(devices, group_size, stage))
        current = kept + received

    pre_share = current[:, : 2 * hidden_units]
    hidden_grad = current[:, 2 * hidden_units :]
    hidden_share = (
        jax.nn.silu(pre_share[:, :hidden_units]) * pre_share[:, hidden_units:]
    ).astype(jnp.bfloat16)
    gate_pre = saved[:, :hidden_units].astype(jnp.float32)
    up_pre = saved[:, hidden_units:].astype(jnp.float32)
    sigmoid_gate = jax.nn.sigmoid(gate_pre)
    gate_grad = hidden_grad * up_pre * sigmoid_gate * (1.0 + gate_pre * (1.0 - sigmoid_gate))
    up_grad = hidden_grad * gate_pre * sigmoid_gate
    current = jnp.concatenate([hidden_share, gate_grad.astype(jnp.bfloat16), up_grad.astype(jnp.bfloat16)], axis=1)

    for stage in reversed(range(1, levels)):
        partner = lax.ppermute(current, "expert", stage_route(devices, group_size, stage))
        current = jnp.concatenate([current, partner], axis=0)

    def last_matmul(block):
        out_down = jnp.dot(
            block[:, :hidden_units], proj_out, preferred_element_type=jnp.float32
        ).astype(jnp.bfloat16)
        out_up = lax.dot_general(
            block[:, hidden_units:], proj_in, (((1,), (1,)), ((), ())),
            preferred_element_type=jnp.float32,
        ).astype(jnp.bfloat16)
        return jnp.stack([out_down, out_up])

    partner = lax.ppermute(current, "expert", stage_route(devices, group_size, 0))
    own_out = last_matmul(current)
    result = jnp.concatenate([own_out, last_matmul(partner)], axis=1)
    neighbour = index ^ 1
    flags = [
        [own_stage_bit(index, group_size, stage), own_stage_bit(neighbour, group_size, stage)]
        for stage in range(levels)
    ]
    sources = []
    for position in range(group_size):
        wanted = [position >> (levels - 1 - level) & 1 for level in range(levels)]
        first = wanted[0] ^ flags[0][0]
        source = first
        for level in range(1, levels):
            flag = jnp.where(first == 1, flags[level][1], flags[level][0])
            source = source * 2 + (wanted[level] ^ flag)
        sources.append(source)
    blocks = result.reshape(2, group_size, -1, share_width)
    result = jnp.take(blocks, jnp.stack(sources), axis=1).reshape(2, -1, share_width)
    result = result.reshape(2, devices, MOST, share_width).transpose(1, 0, 2, 3)
    back = lax.all_to_all(result, "expert", split_axis=0, concat_axis=0, tiled=True)
    back = back.reshape(EXPERTS, group_size, 2, MOST, share_width)
    gathered = jnp.einsum(
        "pkrjt,rhpjc->ptkhc",
        onehot.reshape(2, -1, EXPERTS, MOST, onehot.shape[-1]),
        back,
        preferred_element_type=jnp.float32,
    )
    gathered = gathered.reshape(2, tokens.shape[1], -1, model_width)
    summed = tokens.astype(jnp.float32) + jnp.sum(gates[..., None] * gathered, axis=2)
    summed = summed.astype(jnp.bfloat16)
    return (summed[0][None], summed[1][None])


def solution(mesh):
    placed = (
        P("pipe", "expert", None),
        P("pipe", "expert", None),
        P("pipe", "expert", None),
        P("pipe", "expert", None),
        P("pipe", "expert", None),
        P("pipe", "expert", None),
        P("pipe", "expert", None, None),
        P("pipe", "expert", None, None),
        P("pipe", "expert", None, None),
    )
    return jax.shard_map(
        body,
        mesh=mesh,
        in_specs=placed,
        out_specs=(P("pipe", "expert", None), P("pipe", "expert", None)),
        check_vma=False,
    )
```
